512 devices in a mesh: row: 16 (over x, y), col: 32 (over z, core).
Axes of the slice: x: 4, y: 4, z: 16, core: 2. Of those that a mesh axis runs over, the one named last changes fastest.
Arguments:
- a_tiles: bfloat16 [4096, 16, 128, 128], P(('row', 'col')), may hold values from -0.5 to 0.5
- a_cols: int32 [4096, 16], P(('row', 'col')), may hold values from -1 to 103, as said below
- p_tiles: bfloat16 [4096, 2, 128, 128], P(('row', 'col')), may hold values from -0.375 to 0.375
- p_cols: int32 [4096, 2], P(('row', 'col')), may hold values from 0 to 3, all different within a row
- send_list: int32 [512, 96], P(('row', 'col')), may hold values from 0 to 7
Outputs:
- coarse: float32 [8192, 1536], P(('row', 'col'))
The draws below stay inside these ranges and needn't reach their ends.
Inputs may be any that keep to these rules, and one draw needn't show every extreme that they name: a_cols is -1 for an empty slot, else an index below 104 into the buffer of step one; slot 0 of every block row is live and names the row itself; rows of the first row group never use t = 0 and rows of the last never t = 2; a device holds at most 80 live slots, and some device exactly 80. The 2 entries of a row of p_cols differ.
All inputs are finite; a program needn't handle non-finite values.
Results may differ from the reference program's by a relative error of at most 0.0029.
Values may be sent and summed in bfloat16 or wider, within the bound.
No kernel may reach another device: no remote copies, remote signals or barrier semaphores. Data moves between devices by JAX's collectives and lax.ppermute only.
A program may use at most 64 MiB of HBM per device.

```python
import jax
import jax.numpy as jnp
from jax import lax

BS = 128
FB = 8
KA = 16
KP = 2
CG = 4
KLIVE = 80
NF = 4096
N_ROW = 16
N_COL = 32


def draw_a_cols(key, part):
    device_total = N_ROW * N_COL
    slot_total = FB * KA
    spread = KLIVE - FB
    least_extra = spread * 5 // 9
    extra = jax.random.randint(jax.random.fold_in(key, 11), (device_total,), least_extra, spread + 1)
    busy_device = jax.random.randint(jax.random.fold_in(key, 13), (device_total,), 0, 8) == 0
    chosen = jax.random.randint(jax.random.fold_in(key, 14), (), 0, device_total)
    busy_device = busy_device | (jnp.arange(device_total, dtype=jnp.int32) == chosen)
    live_total = jnp.where(busy_device, KLIVE, FB + extra)
    scores = jax.random.randint(jax.random.fold_in(key, 15), (device_total, slot_total), 0, 2 ** 20)
    slot_pos = jnp.arange(slot_total, dtype=jnp.int32)
    is_diag = slot_pos % KA == 0
    sort_score = jnp.where(is_diag[None, :], -1, scores) * slot_total + slot_pos[None, :]
    ranking = jnp.argsort(jnp.argsort(sort_score, axis=1), axis=1)
    is_live = ranking < live_total[:, None]
    picked = jax.random.randint(jax.random.fold_in(key, 16), (device_total, slot_total), 0, FB + 3 * N_COL)
    group_of = jnp.arange(device_total, dtype=jnp.int32) // N_COL
    ghost_slot = jnp.maximum(picked - FB, 0)
    stream = ghost_slot % 3
    forbidden = (picked >= FB) & ((group_of[:, None] == 0) & (stream == 0) | (group_of[:, None] == N_ROW - 1) & (stream == 2))
    picked = jnp.where(forbidden, picked - stream + 1, picked)
    columns = jnp.where(is_diag[None, :], slot_pos[None, :] // KA, picked)
    columns = jnp.where(is_live, columns, -1)
    return columns.reshape(device_total * FB, KA).astype(jnp.int32)


def place_ends(drawn, key, low, top_value):
    index_at = [jax.random.randint(jax.random.fold_in(key, axis), (), 0, length) for axis, length in enumerate(drawn.shape)]
    longest = drawn.shape.index(max(drawn.shape))
    beside = index_at[:longest] + [(index_at[longest] + 1) % drawn.shape[longest]] + index_at[longest + 1:]
    return drawn.at[tuple(index_at)].set(low).at[tuple(beside)].set(top_value)


def block_levels(stream_key, dims, cuts, low, high):
    factor_of, own = 1.0, jax.random.fold_in(stream_key, 6)
    for position, blocks in cuts:
        heights = jnp.exp(jax.random.uniform(jax.random.fold_in(own, position), (blocks,), jnp.float32, low / len(cuts), high / len(cuts)))
        factor_of = factor_of * jnp.repeat(heights, dims[position] // blocks).reshape([-1 if axis == position else 1 for axis in range(len(dims))])
    return factor_of


def choose_distinct(stream_key, rows, amount, top, lift):
    order = jax.random.permutation(jax.random.fold_in(stream_key, 1), amount)
    favour = order
    for power in range(3):
        favour = favour * favour // amount
    favour = favour * lift // amount
    lots = jax.random.randint(jax.random.fold_in(stream_key, 2), (rows, amount), 0, 4096) + favour
    fixed_rows = jax.random.permutation(jax.random.fold_in(stream_key, 3), rows)[jnp.arange(amount) % rows]
    lots = jnp.where(jnp.arange(rows)[:, None] == fixed_rows[None, :], 1 << 14, lots)
    score = lots * amount + jnp.arange(amount)
    return lax.top_k(score.astype(jnp.int32), top)[1].astype(jnp.int32)


def gaussian(stream_key, shape, scale, most, split=(), kind=jnp.bfloat16):
    factor_of = block_levels(stream_key, shape, split, -0.22, 0.18) if split else 1.0
    array = jax.random.normal(stream_key, shape, jnp.float32) * scale * factor_of
    return jnp.minimum(jnp.maximum(array, -most), most).astype(kind)


def setup_inputs(seed: int = 0) -> dict:
    splits = jax.random.split(jax.random.key(seed), 6)
    return {
        "a_tiles": gaussian(splits[0], (NF, KA, BS, BS), BS ** -0.5, 0.5, ((0, 512),)),
        "a_cols": draw_a_cols(jax.random.fold_in(splits[5], 71), 0),
        "p_tiles": gaussian(splits[2], (NF, KP, BS, BS), (32 * FB) ** -0.5, 0.375, ((0, 512),)),
        "p_cols": choose_distinct(splits[3], NF, CG, KP, 0),
        "send_list": place_ends(jax.random.randint(splits[4], (N_ROW * N_COL, 3 * N_COL), 0, FB), jax.random.fold_in(splits[4], 1), 0, FB - 1).astype(jnp.int32),
    }


def reference(a_tiles, a_cols, p_tiles, p_cols, send_list):
    fine_total = FB * N_ROW * N_COL
    fine_index = jnp.arange(fine_total, dtype=jnp.int32)
    device_of = fine_index // FB
    group_of = device_of // N_COL
    column_of = device_of % N_COL
    is_live = a_cols >= 0
    buffer_slot = jnp.maximum(a_cols, 0)
    is_own = buffer_slot < FB
    ghost_slot = jnp.maximum(buffer_slot - FB, 0)
    source_col = ghost_slot // 3
    stream = ghost_slot % 3
    source_group = group_of[:, None] + stream - 1
    in_range = (source_group >= 0) & (source_group < N_ROW)
    source_device = jnp.clip(source_group, 0, N_ROW - 1) * N_COL + source_col
    listed = send_list[source_device, 3 * column_of[:, None] + stream]
    source_row = jnp.where(is_own, device_of[:, None] * FB + buffer_slot, source_device * FB + listed).astype(jnp.int32)
    weight = (is_live & (is_own | in_range)).astype(jnp.float32)
    offset = jnp.where(is_own, CG, stream * CG).astype(jnp.int32)
    window_ids = jnp.arange(3 * CG, dtype=jnp.int32)
    coarse_ids = jnp.arange(CG, dtype=jnp.int32)

    def group_sum(group):
        def add_block(coarse_acc, block):
            first_row = (group * N_COL + block) * FB
            rows_here = first_row + jnp.arange(FB, dtype=jnp.int32)
            a_block = a_tiles[rows_here].astype(jnp.float32)
            sources = source_row[rows_here]
            p_source = p_tiles[sources].astype(jnp.float32)
            rel_col = offset[rows_here][:, :, None] + p_cols[sources]
            member = (rel_col[..., None] == window_ids).astype(jnp.float32) * weight[rows_here][:, :, None, None]
            tile_prod = jnp.einsum("rkxy,rkpyz->rkpxz", a_block, p_source)
            placed = jnp.einsum("rkpl,rkpxz->rxlz", member, tile_prod)
            product_rows = placed.reshape(FB * BS, 3 * CG * BS).astype(jnp.bfloat16)
            own_member = (p_cols[rows_here][..., None] == coarse_ids).astype(jnp.float32)
            dense_prolong = jnp.einsum("rpm,rpxy->rxmy", own_member, p_tiles[rows_here].astype(jnp.float32))
            dense_prolong = dense_prolong.reshape(FB * BS, CG * BS).astype(jnp.bfloat16)
            update = jnp.dot(dense_prolong.T, product_rows, preferred_element_type=jnp.float32)
            return coarse_acc + update, None

        start_acc = jnp.zeros((CG * BS, 3 * CG * BS), jnp.float32)
        result, unused = lax.scan(add_block, start_acc, jnp.arange(N_COL, dtype=jnp.int32))
        return result

    groups = lax.map(group_sum, jnp.arange(N_ROW, dtype=jnp.int32))
    return groups.reshape(N_ROW * CG * BS, 3 * CG * BS)
```

```python
import functools

import jax
import jax.numpy as jnp
from jax import lax
from jax.experimental import pallas as pl
from jax.experimental.pallas import tpu as pltpu
from jax.sharding import PartitionSpec as P

CG = 4


def from_behind(value, axis, steps):
    count = lax.axis_size(axis)
    leading, last = (max(0, -steps), min(count, count - steps))
    return lax.ppermute(value, axis, [(source, source + steps) for source in range(leading, last)])


def product_kernel(rows, slots, src_ref, live_ref, lcol_ref, pcol_ref, a_ref, b_ref, pt_ref, out_ref, acc_ref):
    bs = a_ref.shape[-1]
    out_ref[...] = jnp.zeros_like(out_ref)
    for i in range(rows):
        acc_ref[...] = jnp.zeros_like(acc_ref)

        def slot(k, carry):
            s = i * slots + k

            @pl.when(live_ref[s] != 0)
            def _():
                src = src_ref[s]
                a = a_ref[i, k]
                for p in range(2):
                    col = pl.multiple_of(lcol_ref[2 * s + p] * bs, bs)
                    acc_ref[:, pl.ds(col, bs)] += jnp.dot(
                        a, b_ref[src, p], preferred_element_type=jnp.float32
                    )

            return carry

        lax.fori_loop(0, slots, slot, 0)
        prod = acc_ref[...].astype(jnp.bfloat16)
        for p in range(2):
            m = pcol_ref[2 * i + p]
            out_ref[m] += jnp.dot(pt_ref[i, p], prod, preferred_element_type=jnp.float32)


def local_product(a_tiles, buffer_tiles, p_t, src, live, lcol, pcol, window):
    rows, slots, bs, _ = a_tiles.shape
    smem = pl.BlockSpec(memory_space=pltpu.SMEM)
    vmem = pl.BlockSpec(memory_space=pltpu.VMEM)
    flops = 2 * rows * slots * 2 * bs ** 3 + 2 * rows * 2 * bs * bs * window * bs
    nbytes = (a_tiles.size + buffer_tiles.size + p_t.size) * 2 + CG * bs * window * bs * 4
    return pl.pallas_call(
        functools.partial(product_kernel, rows, slots),
        out_shape=jax.ShapeDtypeStruct((CG, bs, window * bs), jnp.float32),
        in_specs=[smem, smem, smem, smem, vmem, vmem, vmem],
        out_specs=vmem,
        scratch_shapes=[pltpu.VMEM((bs, window * bs), jnp.float32)],
        compiler_params=pltpu.CompilerParams(vmem_limit_bytes=60 * 1024 * 1024),
        cost_estimate=pl.CostEstimate(flops=flops, bytes_accessed=nbytes, transcendentals=0),
    )(src, live, lcol, pcol, a_tiles, buffer_tiles, p_t)


def body(a_tiles, a_cols, p_tiles, p_cols, send_list):
    col_count = lax.axis_size("col")
    row_count = lax.axis_size("row")
    g = lax.axis_index("row")
    c = lax.axis_index("col")
    own_rows, slot_count = a_cols.shape
    tile_count = p_cols.shape[1]
    block_size = a_tiles.shape[-1]
    window = 3 * CG

    ints = jnp.concatenate([p_cols.reshape(-1), send_list.reshape(-1)])
    all_ints = lax.all_gather(ints, ("row", "col"), tiled=False)
    all_pcols = all_ints[:, : own_rows * tile_count].reshape(-1, own_rows, tile_count)
    all_send = all_ints[:, own_rows * tile_count :]

    group_tiles = lax.all_gather(p_tiles, "col", tiled=True)
    q = jnp.arange(col_count, dtype=jnp.int32)
    my_send = lax.dynamic_slice_in_dim(all_send, g * col_count, col_count, axis=0)

    def pick(t):
        return group_tiles[q * own_rows + my_send[:, 3 * c + t]]

    lower = from_behind(pick(0), "row", 1)
    middle = pick(1)
    upper = from_behind(pick(2), "row", -1)
    buffer_tiles = jnp.concatenate([p_tiles, lower, middle, upper], axis=0)

    stream = jnp.arange(3, dtype=jnp.int32)
    src_group = g + stream - 1
    src_dev = jnp.clip(src_group, 0, row_count - 1)[:, None] * col_count + q[None, :]
    listed = all_send[src_dev, 3 * c + stream[:, None]]
    ghost_cols = all_pcols[src_dev, listed] + CG * stream[:, None, None]
    ghost_ok = jnp.broadcast_to(((src_group >= 0) & (src_group < row_count))[:, None], (3, col_count))
    buffer_cols = jnp.concatenate([p_cols + CG, ghost_cols.reshape(-1, tile_count)], axis=0)
    buffer_ok = jnp.concatenate([jnp.ones((own_rows,), bool), ghost_ok.reshape(-1)])

    b = a_cols.reshape(-1)
    bb = jnp.clip(b, 0, own_rows + 3 * col_count - 1)
    ghost = jnp.maximum(bb - own_rows, 0)
    src = jnp.where(bb < own_rows, bb, own_rows + (ghost % 3) * col_count + ghost // 3)
    live = ((b >= 0) & buffer_ok[src]).astype(jnp.int32)
    lcol = jnp.clip(buffer_cols[src], 0, window - 1).reshape(-1)
    pcol = jnp.clip(p_cols, 0, CG - 1).reshape(-1)
    p_t = jnp.swapaxes(p_tiles, -1, -2)
    partial = local_product(a_tiles, buffer_tiles, p_t, src, live, lcol, pcol, window)
    return lax.psum_scatter(
        partial.reshape(CG * block_size, window * block_size),
        "col",
        scatter_dimension=0,
        tiled=True,
    )


def solution(mesh):
    in_specs = (
        P(("row", "col"), None, None, None),
        P(("row", "col"), None),
        P(("row", "col"), None, None, None),
        P(("row", "col"), None),
        P(("row", "col"), None),
    )
    out_specs = P(("row", "col"), None)
    return jax.shard_map(body, mesh=mesh, in_specs=in_specs, out_specs=out_specs, check_vma=False)
```

```python
import functools

import jax
import jax.numpy as jnp
from jax import lax
from jax.experimental import pallas as pl
from jax.experimental.pallas import tpu as pltpu
from jax.sharding import PartitionSpec as P

CG = 4
VMEM_LIMIT = 60 * 1024 * 1024


def from_behind(value, axis, steps):
    count = lax.axis_size(axis)
    leading, last = (max(0, -steps), min(count, count - steps))
    return lax.ppermute(value, axis, [(source, source + steps) for source in range(leading, last)])


def accumulate_rows(rows, slots, src_ref, live_ref, lcol_ref, pcol_ref, a_ref, b_ref, pt_ref, out_ref, acc_ref):
    bs = a_ref.shape[-1]
    out_ref[...] = jnp.zeros_like(out_ref)
    for i in range(rows):
        acc_ref[...] = jnp.zeros_like(acc_ref)

        def slot(k, carry):
            s = i * slots + k

            @pl.when(live_ref[s] != 0)
            def _():
                src = src_ref[s]
                a = a_ref[i, k]
                for p in range(2):
                    col = pl.multiple_of(lcol_ref[2 * s + p] * bs, bs)
                    acc_ref[:, pl.ds(col, bs)] += jnp.dot(
                        a, b_ref[src, p], preferred_element_type=jnp.float32
                    )

            return carry

        lax.fori_loop(0, slots, slot, 0)
        prod = acc_ref[...].astype(jnp.bfloat16)
        for p in range(2):
            m = pcol_ref[2 * i + p]
            out_ref[m] += jnp.dot(pt_ref[i, p], prod, preferred_element_type=jnp.float32)


def middle_kernel(rows, slots, src_ref, live_ref, lcol_ref, pcol_ref, sel_ref, a_ref, group_ref, pt_ref, out_ref, buf_ref, acc_ref, sems):
    own = buf_ref.shape[0] - sel_ref.shape[0]
    me = lax.axis_index("col")
    copies = [pltpu.make_async_copy(group_ref.at[pl.ds(me * own, own)], buf_ref.at[pl.ds(0, own)], sems.at[0])]
    for q in range(sel_ref.shape[0]):
        copies.append(
            pltpu.make_async_copy(group_ref.at[sel_ref[q]], buf_ref.at[own + q], sems.at[q + 1])
        )
    for cp in copies:
        cp.start()
    for cp in copies:
        cp.wait()
    accumulate_rows(rows, slots, src_ref, live_ref, lcol_ref, pcol_ref, a_ref, buf_ref, pt_ref, out_ref, acc_ref)


def side_kernel(rows, slots, src_ref, live_ref, lcol_ref, pcol_ref, a_ref, lower_ref, upper_ref, pt_ref, out_ref, buf_ref, acc_ref, sems):
    half = lower_ref.shape[0]
    copies = [
        pltpu.make_async_copy(lower_ref, buf_ref.at[pl.ds(0, half)], sems.at[0]),
        pltpu.make_async_copy(upper_ref, buf_ref.at[pl.ds(half, half)], sems.at[1]),
    ]
    for cp in copies:
        cp.start()
    for cp in copies:
        cp.wait()
    accumulate_rows(rows, slots, src_ref, live_ref, lcol_ref, pcol_ref, a_ref, buf_ref, pt_ref, out_ref, acc_ref)


def pick_kernel(up_sel, down_sel, group_ref, up_ref, down_ref, sems):
    count = up_sel.shape[0]
    copies = []
    for q in range(count):
        copies.append(pltpu.make_async_copy(group_ref.at[up_sel[q]], up_ref.at[q], sems.at[q]))
        copies.append(
            pltpu.make_async_copy(group_ref.at[down_sel[q]], down_ref.at[q], sems.at[count + q])
        )
    for cp in copies:
        cp.start()
    for cp in copies:
        cp.wait()


SMEM = pl.BlockSpec(memory_space=pltpu.SMEM)
VMEM = pl.BlockSpec(memory_space=pltpu.VMEM)
ANY = pl.BlockSpec(memory_space=pl.ANY)


def cost(a_tiles, width, extra_bytes):
    rows, slots, bs, _ = a_tiles.shape
    flops = 2 * rows * slots * 2 * bs ** 3 + 2 * rows * 2 * bs * bs * width * bs
    return pl.CostEstimate(
        flops=flops,
        bytes_accessed=a_tiles.size * 2 + extra_bytes + CG * bs * width * bs * 4,
        transcendentals=0,
    )


def middle_product(a_tiles, group_tiles, p_t, sel, src, live, lcol, pcol):
    rows, slots, bs, _ = a_tiles.shape
    count = sel.shape[0]
    width = CG
    return pl.pallas_call(
        functools.partial(middle_kernel, rows, slots),
        out_shape=jax.ShapeDtypeStruct((CG, bs, width * bs), jnp.float32),
        in_specs=[SMEM, SMEM, SMEM, SMEM, SMEM, VMEM, ANY, VMEM],
        out_specs=VMEM,
        scratch_shapes=[
            pltpu.VMEM((rows + count, 2, bs, bs), jnp.bfloat16),
            pltpu.VMEM((bs, width * bs), jnp.float32),
            pltpu.SemaphoreType.DMA((count + 1,)),
        ],
        compiler_params=pltpu.CompilerParams(vmem_limit_bytes=VMEM_LIMIT),
        cost_estimate=cost(a_tiles, width, (rows + count) * 2 * bs * bs * 2),
    )(src, live, lcol, pcol, sel, a_tiles, group_tiles, p_t)


def side_product(a_tiles, lower, upper, p_t, src, live, lcol, pcol):
    rows, slots, bs, _ = a_tiles.shape
    count = lower.shape[0]
    width = 2 * CG
    return pl.pallas_call(
        functools.partial(side_kernel, rows, slots),
        out_shape=jax.ShapeDtypeStruct((CG, bs, width * bs), jnp.float32),
        in_specs=[SMEM, SMEM, SMEM, SMEM, VMEM, ANY, ANY, VMEM],
        out_specs=VMEM,
        scratch_shapes=[
            pltpu.VMEM((2 * count, 2, bs, bs), jnp.bfloat16),
            pltpu.VMEM((bs, width * bs), jnp.float32),
            pltpu.SemaphoreType.DMA((2,)),
        ],
        compiler_params=pltpu.CompilerParams(vmem_limit_bytes=VMEM_LIMIT),
        cost_estimate=cost(a_tiles, width, 2 * count * 2 * bs * bs * 2),
    )(src, live, lcol, pcol, a_tiles, lower, upper, p_t)


def pick_rows(group_tiles, up_sel, down_sel):
    count = up_sel.shape[0]
    shape = (count,) + group_tiles.shape[1:]
    out = jax.ShapeDtypeStruct(shape, group_tiles.dtype)
    nbytes = 2 * 2 * count * group_tiles[0].size * 2
    return pl.pallas_call(
        pick_kernel,
        out_shape=(out, out),
        in_specs=[SMEM, SMEM, ANY],
        out_specs=(VMEM, VMEM),
        scratch_shapes=[pltpu.SemaphoreType.DMA((2 * count,))],
        compiler_params=pltpu.CompilerParams(vmem_limit_bytes=VMEM_LIMIT),
        cost_estimate=pl.CostEstimate(flops=0, bytes_accessed=nbytes, transcendentals=0),
    )(up_sel, down_sel, group_tiles)


def body(a_tiles, a_cols, p_tiles, p_cols, send_list):
    col_count = lax.axis_size("col")
    row_count = lax.axis_size("row")
    g = lax.axis_index("row")
    c = lax.axis_index("col")
    own_rows, slot_count = a_cols.shape
    tile_count = p_cols.shape[1]
    block_size = a_tiles.shape[-1]

    ints = jnp.concatenate([p_cols.reshape(-1), send_list.reshape(-1)])
    group_ints = lax.all_gather(ints, "col", tiled=False)
    group_pcols = group_ints[:, : own_rows * tile_count].reshape(-1, tile_count)
    group_send = group_ints[:, own_rows * tile_count :]
    group_tiles = lax.all_gather(p_tiles, "col", tiled=True)

    q = jnp.arange(col_count, dtype=jnp.int32)

    def selection(t):
        return q * own_rows + jnp.clip(group_send[:, 3 * c + t], 0, own_rows - 1)

    up_sel, mid_sel, down_sel = selection(0), selection(1), selection(2)
    up_tiles, down_tiles = pick_rows(group_tiles, up_sel, down_sel)
    lower_tiles, lower_cols = from_behind((up_tiles, group_pcols[up_sel]), "row", 1)
    upper_tiles, upper_cols = from_behind((down_tiles, group_pcols[down_sel]), "row", -1)
    mid_cols = group_pcols[mid_sel]

    b = a_cols.reshape(-1)
    live = b >= 0
    bb = jnp.clip(b, 0, own_rows + 3 * col_count - 1)
    is_own = bb < own_rows
    ghost = jnp.maximum(bb - own_rows, 0)
    ghost_q = ghost // 3
    stream = ghost % 3
    src_group = g + stream - 1
    in_range = (src_group >= 0) & (src_group < row_count)
    pcol = jnp.clip(p_cols, 0, CG - 1)

    mid_src = jnp.where(is_own, bb, own_rows + ghost_q)
    mid_live = (live & (is_own | (stream == 1))).astype(jnp.int32)
    mid_table = jnp.concatenate([pcol, jnp.clip(mid_cols, 0, CG - 1)], axis=0)
    mid_lcol = mid_table[mid_src].reshape(-1)

    side_src = jnp.where(stream == 0, ghost_q, col_count + ghost_q)
    side_live = (live & ~is_own & (stream != 1) & in_range).astype(jnp.int32)
    side_table = jnp.concatenate(
        [jnp.clip(lower_cols, 0, CG - 1), jnp.clip(upper_cols, 0, CG - 1) + CG], axis=0
    )
    side_lcol = side_table[side_src].reshape(-1)

    p_t = jnp.swapaxes(p_tiles, -1, -2)
    pcol = pcol.reshape(-1)
    mid = middle_product(a_tiles, group_tiles, p_t, mid_sel, mid_src, mid_live, mid_lcol, pcol)
    mid = lax.psum_scatter(
        mid.reshape(CG * block_size, CG * block_size), "col", scatter_dimension=0, tiled=True
    )
    side = side_product(
        a_tiles, lower_tiles, upper_tiles, p_t, side_src, side_live, side_lcol, pcol
    )
    side = lax.psum_scatter(
        side.reshape(CG * block_size, 2 * CG * block_size), "col", scatter_dimension=0, tiled=True
    )
    width = CG * block_size
    return jnp.concatenate([side[:, :width], mid, side[:, width:]], axis=1)


def solution(mesh):
    in_specs = (
        P(("row", "col"), None, None, None),
        P(("row", "col"), None),
        P(("row", "col"), None, None, None),
        P(("row", "col"), None),
        P(("row", "col"), None),
    )
    out_specs = P(("row", "col"), None)
    return jax.shard_map(body, mesh=mesh, in_specs=in_specs, out_specs=out_specs, check_vma=False)
```

```python
import functools

import jax
import jax.numpy as jnp
from jax import lax
from jax.experimental import pallas as pl
from jax.experimental.pallas import tpu as pltpu
from jax.sharding import PartitionSpec as P

CG = 4
VMEM_LIMIT = 60 * 1024 * 1024


def from_behind(value, axis, steps):
    count = lax.axis_size(axis)
    leading, last = (max(0, -steps), min(count, count - steps))
    return lax.ppermute(value, axis, [(source, source + steps) for source in range(leading, last)])


def accumulate_rows(rows, slots, src_ref, live_ref, lcol_ref, pcol_ref, a_ref, b_ref, pt_ref, out_ref, acc_ref):
    bs = a_ref.shape[-1]
    for i in range(rows):
        acc_ref[...] = jnp.zeros_like(acc_ref)

        def slot(k, carry):
            s = i * slots + k

            @pl.when(live_ref[s] != 0)
            def _():
                src = src_ref[s]
                a = a_ref[i, k]
                for p in range(2):
                    col = pl.multiple_of(lcol_ref[2 * s + p] * bs, bs)
                    acc_ref[:, pl.ds(col, bs)] += jnp.dot(
                        a, b_ref[src, p], preferred_element_type=jnp.float32
                    )

            return carry

        lax.fori_loop(0, slots, slot, 0)
        prod = acc_ref[...].astype(jnp.bfloat16)
        for p in range(2):
            m = pcol_ref[2 * i + p]
            out_ref[m] += jnp.dot(pt_ref[i, p], prod, preferred_element_type=jnp.float32)


def middle_kernel(rows, slots, src_ref, live_ref, lcol_ref, pcol_ref, sel_ref, a_ref, group_ref, pt_ref, out_ref, buf_ref, acc_ref, sems):
    own = buf_ref.shape[0] - sel_ref.shape[0]
    me = lax.axis_index("core") * lax.axis_size("z") + lax.axis_index("z")
    copies = [pltpu.make_async_copy(group_ref.at[pl.ds(me * own, own)], buf_ref.at[pl.ds(0, own)], sems.at[0])]
    for q in range(sel_ref.shape[0]):
        copies.append(
            pltpu.make_async_copy(group_ref.at[sel_ref[q]], buf_ref.at[own + q], sems.at[q + 1])
        )
    for cp in copies:
        cp.start()
    out_ref[...] = jnp.zeros_like(out_ref)
    for cp in copies:
        cp.wait()
    accumulate_rows(rows, slots, src_ref, live_ref, lcol_ref, pcol_ref, a_ref, buf_ref, pt_ref, out_ref, acc_ref)


def side_kernel(rows, slots, src_ref, live_ref, lcol_ref, pcol_ref, a_ref, lower_ref, upper_ref, pt_ref, prior_ref, out_ref, buf_ref, acc_ref, sems):
    half = lower_ref.shape[0]
    copies = [
        pltpu.make_async_copy(lower_ref, buf_ref.at[pl.ds(0, half)], sems.at[0]),
        pltpu.make_async_copy(upper_ref, buf_ref.at[pl.ds(half, half)], sems.at[1]),
    ]
    for cp in copies:
        cp.start()
    out_ref[...] = prior_ref[...]
    for cp in copies:
        cp.wait()
    accumulate_rows(rows, slots, src_ref, live_ref, lcol_ref, pcol_ref, a_ref, buf_ref, pt_ref, out_ref, acc_ref)


def pick_kernel(up_sel, down_sel, group_ref, up_ref, down_ref, sems):
    count = up_sel.shape[0]
    copies = []
    for q in range(count):
        copies.append(pltpu.make_async_copy(group_ref.at[up_sel[q]], up_ref.at[q], sems.at[q]))
        copies.append(
            pltpu.make_async_copy(group_ref.at[down_sel[q]], down_ref.at[q], sems.at[count + q])
        )
    for cp in copies:
        cp.start()
    for cp in copies:
        cp.wait()


SMEM = pl.BlockSpec(memory_space=pltpu.SMEM)
VMEM = pl.BlockSpec(memory_space=pltpu.VMEM)
ANY = pl.BlockSpec(memory_space=pl.ANY)


def cost(a_tiles, width, extra_bytes):
    rows, slots, bs, _ = a_tiles.shape
    flops = 2 * rows * slots * 2 * bs ** 3 + 2 * rows * 2 * bs * bs * width * bs
    return pl.CostEstimate(
        flops=flops,
        bytes_accessed=a_tiles.size * 2 + extra_bytes + CG * bs * width * bs * 4,
        transcendentals=0,
    )


def middle_product(a_tiles, group_tiles, p_t, sel, src, live, lcol, pcol):
    rows, slots, bs, _ = a_tiles.shape
    count = sel.shape[0]
    width = 3 * CG
    return pl.pallas_call(
        functools.partial(middle_kernel, rows, slots),
        out_shape=jax.ShapeDtypeStruct((CG, bs, width * bs), jnp.float32),
        in_specs=[SMEM, SMEM, SMEM, SMEM, SMEM, VMEM, ANY, VMEM],
        out_specs=VMEM,
        scratch_shapes=[
            pltpu.VMEM((rows + count, 2, bs, bs), jnp.bfloat16),
            pltpu.VMEM((bs, width * bs), jnp.float32),
            pltpu.SemaphoreType.DMA((count + 1,)),
        ],
        compiler_params=pltpu.CompilerParams(vmem_limit_bytes=VMEM_LIMIT),
        cost_estimate=cost(a_tiles, width, (rows + count) * 2 * bs * bs * 2),
    )(src, live, lcol, pcol, sel, a_tiles, group_tiles, p_t)


def side_product(a_tiles, lower, upper, p_t, src, live, lcol, pcol, prior):
    rows, slots, bs, _ = a_tiles.shape
    count = lower.shape[0]
    width = 3 * CG
    return pl.pallas_call(
        functools.partial(side_kernel, rows, slots),
        out_shape=jax.ShapeDtypeStruct((CG, bs, width * bs), jnp.float32),
        in_specs=[SMEM, SMEM, SMEM, SMEM, VMEM, ANY, ANY, VMEM, VMEM],
        input_output_aliases={8: 0},
        out_specs=VMEM,
        scratch_shapes=[
            pltpu.VMEM((2 * count, 2, bs, bs), jnp.bfloat16),
            pltpu.VMEM((bs, width * bs), jnp.float32),
            pltpu.SemaphoreType.DMA((2,)),
        ],
        compiler_params=pltpu.CompilerParams(vmem_limit_bytes=VMEM_LIMIT),
        cost_estimate=cost(a_tiles, width, 2 * count * 2 * bs * bs * 2),
    )(src, live, lcol, pcol, a_tiles, lower, upper, p_t, prior)


def pick_rows(group_tiles, up_sel, down_sel):
    count = up_sel.shape[0]
    shape = (count,) + group_tiles.shape[1:]
    out = jax.ShapeDtypeStruct(shape, group_tiles.dtype)
    nbytes = 2 * 2 * count * group_tiles[0].size * 2
    return pl.pallas_call(
        pick_kernel,
        out_shape=(out, out),
        in_specs=[SMEM, SMEM, ANY],
        out_specs=(VMEM, VMEM),
        scratch_shapes=[pltpu.SemaphoreType.DMA((2 * count,))],
        compiler_params=pltpu.CompilerParams(vmem_limit_bytes=VMEM_LIMIT),
        cost_estimate=pl.CostEstimate(flops=0, bytes_accessed=nbytes, transcendentals=0),
    )(up_sel, down_sel, group_tiles)


def body(a_tiles, a_cols, p_tiles, p_cols, send_list):
    z_count = lax.axis_size("z")
    core_count = lax.axis_size("core")
    col_count = z_count * core_count
    row_count = lax.axis_size("row")
    g = lax.axis_index("row")
    c = lax.axis_index("z") * core_count + lax.axis_index("core")
    own_rows, slot_count = a_cols.shape
    tile_count = p_cols.shape[1]
    block_size = a_tiles.shape[-1]

    ints = jnp.concatenate([p_cols.reshape(-1), send_list.reshape(-1)])
    group_ints = lax.all_gather(lax.all_gather(ints, "z"), "core")
    group_ints = jnp.swapaxes(group_ints, 0, 1).reshape(col_count, -1)
    group_pcols = group_ints[:, : own_rows * tile_count].reshape(-1, tile_count)
    group_send = group_ints[:, own_rows * tile_count :]
    group_tiles = lax.all_gather(lax.all_gather(p_tiles, "z", tiled=True), "core", tiled=True)

    q = jnp.arange(col_count, dtype=jnp.int32)
    base = ((q % core_count) * z_count + q // core_count) * own_rows

    def selection(t):
        return base + jnp.clip(group_send[:, 3 * c + t], 0, own_rows - 1)

    up_sel, mid_sel, down_sel = selection(0), selection(1), selection(2)
    up_tiles, down_tiles = pick_rows(group_tiles, up_sel, down_sel)

    def cols_of(t):
        return group_pcols[q * own_rows + jnp.clip(group_send[:, 3 * c + t], 0, own_rows - 1)]

    lower_tiles, lower_cols = from_behind((up_tiles, cols_of(0)), "row", 1)
    upper_tiles, upper_cols = from_behind((down_tiles, cols_of(2)), "row", -1)
    mid_cols = cols_of(1)

    b = a_cols.reshape(-1)
    live = b >= 0
    bb = jnp.clip(b, 0, own_rows + 3 * col_count - 1)
    is_own = bb < own_rows
    ghost = jnp.maximum(bb - own_rows, 0)
    ghost_q = ghost // 3
    stream = ghost % 3
    src_group = g + stream - 1
    in_range = (src_group >= 0) & (src_group < row_count)
    pcol = jnp.clip(p_cols, 0, CG - 1)

    mid_src = jnp.where(is_own, bb, own_rows + ghost_q)
    mid_live = (live & (is_own | (stream == 1))).astype(jnp.int32)
    mid_table = jnp.concatenate([pcol, jnp.clip(mid_cols, 0, CG - 1)], axis=0) + CG
    mid_lcol = mid_table[mid_src].reshape(-1)

    side_src = jnp.where(stream == 0, ghost_q, col_count + ghost_q)
    side_live = (live & ~is_own & (stream != 1) & in_range).astype(jnp.int32)
    side_table = jnp.concatenate(
        [jnp.clip(lower_cols, 0, CG - 1), jnp.clip(upper_cols, 0, CG - 1) + 2 * CG], axis=0
    )
    side_lcol = side_table[side_src].reshape(-1)

    p_t = jnp.swapaxes(p_tiles, -1, -2)
    pcol = pcol.reshape(-1)
    mid = middle_product(a_tiles, group_tiles, p_t, mid_sel, mid_src, mid_live, mid_lcol, pcol)
    partial = side_product(
        a_tiles, lower_tiles, upper_tiles, p_t, side_src, side_live, side_lcol, pcol, mid
    )
    partial = partial.reshape(CG * block_size, 3 * CG * block_size)
    partial = lax.psum_scatter(partial, "z", scatter_dimension=0, tiled=True)
    return lax.psum_scatter(partial, "core", scatter_dimension=0, tiled=True)


def solution(mesh):
    rows, cols = mesh.devices.shape
    chip_mesh = jax.sharding.Mesh(mesh.devices.reshape(rows, cols // 2, 2), ("row", "z", "core"))
    split = ("row", "z", "core")
    in_specs = (
        P(split, None, None, None),
        P(split, None),
        P(split, None, None, None),
        P(split, None),
        P(split, None),
    )
    out_specs = P(split, None)
    return jax.shard_map(body, mesh=chip_mesh, in_specs=in_specs, out_specs=out_specs, check_vma=False)
```

```python
import functools

import jax
import jax.numpy as jnp
from jax import lax
from jax.experimental import pallas as pl
from jax.experimental.pallas import tpu as pltpu
from jax.sharding import PartitionSpec as P

CG = 4
VMEM_LIMIT = 60 * 1024 * 1024


def from_behind(value, axis, steps):
    count = lax.axis_size(axis)
    leading, last = (max(0, -steps), min(count, count - steps))
    return lax.ppermute(value, axis, [(source, source + steps) for source in range(leading, last)])


def accumulate_rows(rows, slots, spans, src_ref, live_ref, lcol_ref, pcol_ref, a_ref, b_ref, pt_ref, out_ref, acc_ref):
    bs = a_ref.shape[-1]
    for i in range(rows):
        acc_ref[...] = jnp.zeros_like(acc_ref)

        def slot(k, carry):
            s = i * slots + k

            @pl.when(live_ref[s] != 0)
            def _():
                src = src_ref[s]
                a = a_ref[i, k]
                for p in range(2):
                    col = pl.multiple_of(lcol_ref[2 * s + p] * bs, bs)
                    acc_ref[:, pl.ds(col, bs)] += jnp.dot(
                        a, b_ref[src, p], preferred_element_type=jnp.float32
                    )

            return carry

        lax.fori_loop(0, slots, slot, 0)
        for lo, hi in spans:
            prod = acc_ref[:, lo * bs : hi * bs].astype(jnp.bfloat16)
            for p in range(2):
                m = pcol_ref[2 * i + p]
                out_ref[m, :, lo * bs : hi * bs] += jnp.dot(
                    pt_ref[i, p], prod, preferred_element_type=jnp.float32
                )


def middle_kernel(rows, slots, src_ref, live_ref, lcol_ref, pcol_ref, sel_ref, a_ref, group_ref, pt_ref, out_ref, buf_ref, acc_ref, sems):
    own = buf_ref.shape[0] - sel_ref.shape[0]
    me = lax.axis_index("z") * lax.axis_size("core") + lax.axis_index("core")
    copies = [pltpu.make_async_copy(group_ref.at[pl.ds(me * own, own)], buf_ref.at[pl.ds(0, own)], sems.at[0])]
    for q in range(sel_ref.shape[0]):
        copies.append(
            pltpu.make_async_copy(group_ref.at[sel_ref[q]], buf_ref.at[own + q], sems.at[q + 1])
        )
    for cp in copies:
        cp.start()
    out_ref[...] = jnp.zeros_like(out_ref)
    for cp in copies:
        cp.wait()
    spans = ((CG, 2 * CG),)
    accumulate_rows(rows, slots, spans, src_ref, live_ref, lcol_ref, pcol_ref, a_ref, buf_ref, pt_ref, out_ref, acc_ref)


def side_kernel(rows, slots, src_ref, live_ref, lcol_ref, pcol_ref, a_ref, lower_ref, upper_ref, pt_ref, prior_ref, out_ref, buf_ref, acc_ref, sems):
    half = lower_ref.shape[0]
    copies = [
        pltpu.make_async_copy(lower_ref, buf_ref.at[pl.ds(0, half)], sems.at[0]),
        pltpu.make_async_copy(upper_ref, buf_ref.at[pl.ds(half, half)], sems.at[1]),
    ]
    for cp in copies:
        cp.start()
    out_ref[...] = prior_ref[...]
    for cp in copies:
        cp.wait()
    spans = ((0, CG), (2 * CG, 3 * CG))
    accumulate_rows(rows, slots, spans, src_ref, live_ref, lcol_ref, pcol_ref, a_ref, buf_ref, pt_ref, out_ref, acc_ref)


def pick_kernel(up_sel, down_sel, group_ref, up_ref, down_ref, sems):
    count = up_sel.shape[0]
    copies = []
    for q in range(count):
        copies.append(pltpu.make_async_copy(group_ref.at[up_sel[q]], up_ref.at[q], sems.at[q]))
        copies.append(
            pltpu.make_async_copy(group_ref.at[down_sel[q]], down_ref.at[q], sems.at[count + q])
        )
    for cp in copies:
        cp.start()
    for cp in copies:
        cp.wait()


SMEM = pl.BlockSpec(memory_space=pltpu.SMEM)
VMEM = pl.BlockSpec(memory_space=pltpu.VMEM)
ANY = pl.BlockSpec(memory_space=pl.ANY)


def cost(a_tiles, width, extra_bytes):
    rows, slots, bs, _ = a_tiles.shape
    flops = 2 * rows * slots * 2 * bs ** 3 + 2 * rows * 2 * bs * bs * width * bs
    return pl.CostEstimate(
        flops=flops,
        bytes_accessed=a_tiles.size * 2 + extra_bytes + CG * bs * width * bs * 4,
        transcendentals=0,
    )


def middle_product(a_tiles, group_tiles, p_t, sel, src, live, lcol, pcol):
    rows, slots, bs, _ = a_tiles.shape
    count = sel.shape[0]
    width = 3 * CG
    return pl.pallas_call(
        functools.partial(middle_kernel, rows, slots),
        out_shape=jax.ShapeDtypeStruct((CG, bs, width * bs), jnp.float32),
        in_specs=[SMEM, SMEM, SMEM, SMEM, SMEM, VMEM, ANY, VMEM],
        out_specs=VMEM,
        scratch_shapes=[
            pltpu.VMEM((rows + count, 2, bs, bs), jnp.bfloat16),
            pltpu.VMEM((bs, width * bs), jnp.float32),
            pltpu.SemaphoreType.DMA((count + 1,)),
        ],
        compiler_params=pltpu.CompilerParams(vmem_limit_bytes=VMEM_LIMIT),
        cost_estimate=cost(a_tiles, width, (rows + count) * 2 * bs * bs * 2),
    )(src, live, lcol, pcol, sel, a_tiles, group_tiles, p_t)


def side_product(a_tiles, lower, upper, p_t, src, live, lcol, pcol, prior):
    rows, slots, bs, _ = a_tiles.shape
    count = lower.shape[0]
    width = 3 * CG
    return pl.pallas_call(
        functools.partial(side_kernel, rows, slots),
        out_shape=jax.ShapeDtypeStruct((CG, bs, width * bs), jnp.float32),
        in_specs=[SMEM, SMEM, SMEM, SMEM, VMEM, ANY, ANY, VMEM, VMEM],
        input_output_aliases={8: 0},
        out_specs=VMEM,
        scratch_shapes=[
            pltpu.VMEM((2 * count, 2, bs, bs), jnp.bfloat16),
            pltpu.VMEM((bs, width * bs), jnp.float32),
            pltpu.SemaphoreType.DMA((2,)),
        ],
        compiler_params=pltpu.CompilerParams(vmem_limit_bytes=VMEM_LIMIT),
        cost_estimate=cost(a_tiles, width, 2 * count * 2 * bs * bs * 2),
    )(src, live, lcol, pcol, a_tiles, lower, upper, p_t, prior)


def pick_rows(group_tiles, up_sel, down_sel):
    count = up_sel.shape[0]
    shape = (count,) + group_tiles.shape[1:]
    out = jax.ShapeDtypeStruct(shape, group_tiles.dtype)
    nbytes = 2 * 2 * count * group_tiles[0].size * 2
    return pl.pallas_call(
        pick_kernel,
        out_shape=(out, out),
        in_specs=[SMEM, SMEM, ANY],
        out_specs=(VMEM, VMEM),
        scratch_shapes=[pltpu.SemaphoreType.DMA((2 * count,))],
        compiler_params=pltpu.CompilerParams(vmem_limit_bytes=VMEM_LIMIT),
        cost_estimate=pl.CostEstimate(flops=0, bytes_accessed=nbytes, transcendentals=0),
    )(up_sel, down_sel, group_tiles)


def body(a_tiles, a_cols, p_tiles, p_cols, send_list):
    z_count = lax.axis_size("z")
    core_count = lax.axis_size("core")
    col_count = z_count * core_count
    row_count = lax.axis_size("row")
    g = lax.axis_index("row")
    c = lax.axis_index("z") * core_count + lax.axis_index("core")
    own_rows, slot_count = a_cols.shape
    tile_count = p_cols.shape[1]
    block_size = a_tiles.shape[-1]

    ints = jnp.concatenate([p_cols.reshape(-1), send_list.reshape(-1)])
    group_ints = lax.all_gather(ints, ("z", "core"))
    group_pcols = group_ints[:, : own_rows * tile_count].reshape(-1, tile_count)
    group_send = group_ints[:, own_rows * tile_count :]
    group_tiles = lax.all_gather(p_tiles, ("z", "core"), tiled=True)

    q = jnp.arange(col_count, dtype=jnp.int32)
    base = q * own_rows

    def selection(t):
        return base + jnp.clip(group_send[:, 3 * c + t], 0, own_rows - 1)

    up_sel, mid_sel, down_sel = selection(0), selection(1), selection(2)
    up_tiles, down_tiles = pick_rows(group_tiles, up_sel, down_sel)

    def cols_of(t):
        return group_pcols[q * own_rows + jnp.clip(group_send[:, 3 * c + t], 0, own_rows - 1)]

    lower_tiles, lower_cols = from_behind((up_tiles, cols_of(0)), "row", 1)
    upper_tiles, upper_cols = from_behind((down_tiles, cols_of(2)), "row", -1)
    mid_cols = cols_of(1)

    b = a_cols.reshape(-1)
    live = b >= 0
    bb = jnp.clip(b, 0, own_rows + 3 * col_count - 1)
    is_own = bb < own_rows
    ghost = jnp.maximum(bb - own_rows, 0)
    ghost_q = ghost // 3
    stream = ghost % 3
    src_group = g + stream - 1
    in_range = (src_group >= 0) & (src_group < row_count)
    pcol = jnp.clip(p_cols, 0, CG - 1)

    mid_src = jnp.where(is_own, bb, own_rows + ghost_q)
    mid_live = (live & (is_own | (stream == 1))).astype(jnp.int32)
    mid_table = jnp.concatenate([pcol, jnp.clip(mid_cols, 0, CG - 1)], axis=0) + CG
    mid_lcol = mid_table[mid_src].reshape(-1)

    side_src = jnp.where(stream == 0, ghost_q, col_count + ghost_q)
    side_live = (live & ~is_own & (stream != 1) & in_range).astype(jnp.int32)
    side_table = jnp.concatenate(
        [jnp.clip(lower_cols, 0, CG - 1), jnp.clip(upper_cols, 0, CG - 1) + 2 * CG], axis=0
    )
    side_lcol = side_table[side_src].reshape(-1)

    p_t = jnp.swapaxes(p_tiles, -1, -2)
    pcol = pcol.reshape(-1)
    mid = middle_product(a_tiles, group_tiles, p_t, mid_sel, mid_src, mid_live, mid_lcol, pcol)
    partial = side_product(
        a_tiles, lower_tiles, upper_tiles, p_t, side_src, side_live, side_lcol, pcol, mid
    )
    partial = partial.reshape(CG * block_size, 3 * CG * block_size)
    partial = lax.psum_scatter(partial, "z", scatter_dimension=0, tiled=True)
    return lax.psum_scatter(partial, "core", scatter_dimension=0, tiled=True)


def solution(mesh):
    rows, cols = mesh.devices.shape
    chip_mesh = jax.sharding.Mesh(mesh.devices.reshape(rows, cols // 2, 2), ("row", "z", "core"))
    split = ("row", "z", "core")
    in_specs = (
        P(split, None, None, None),
        P(split, None),
        P(split, None, None, None),
        P(split, None),
        P(split, None),
    )
    out_specs = P(split, None)
    return jax.shard_map(body, mesh=chip_mesh, in_specs=in_specs, out_specs=out_specs, check_vma=False)
```

```python
import functools

import jax
import jax.numpy as jnp
from jax import lax
from jax.experimental import pallas as pl
from jax.experimental.pallas import tpu as pltpu
from jax.sharding import PartitionSpec as P

CG = 4
VMEM_LIMIT = 60 * 1024 * 1024


def from_behind(value, axis, steps):
    count = lax.axis_size(axis)
    leading, last = (max(0, -steps), min(count, count - steps))
    return lax.ppermute(value, axis, [(source, source + steps) for source in range(leading, last)])


def accumulate_rows(rows, slots, spans, src_ref, live_ref, lcol_ref, pcol_ref, a_ref, b_ref, pt_ref, out_ref, acc_ref):
    bs = a_ref.shape[-1]
    for i in range(rows):
        for lo, hi in spans:
            acc_ref[:, lo * bs : hi * bs] = jnp.zeros((bs, (hi - lo) * bs), jnp.float32)

        def slot(k, carry):
            s = i * slots + k

            @pl.when(live_ref[s] != 0)
            def _():
                src = src_ref[s]
                a = a_ref[i, k]
                for p in range(2):
                    col = pl.multiple_of(lcol_ref[2 * s + p] * bs, bs)
                    acc_ref[:, pl.ds(col, bs)] += jnp.dot(
                        a, b_ref[src, p], preferred_element_type=jnp.float32
                    )

            return carry

        lax.fori_loop(0, slots, slot, 0)
        for lo, hi in spans:
            prod = acc_ref[:, lo * bs : hi * bs].astype(jnp.bfloat16)
            for p in range(2):
                m = pcol_ref[2 * i + p]
                out_ref[m, :, lo * bs : hi * bs] += jnp.dot(
                    pt_ref[i, p], prod, preferred_element_type=jnp.float32
                )


def middle_kernel(rows, slots, src_ref, live_ref, lcol_ref, pcol_ref, sel_ref, a_ref, group_ref, pt_ref, out_ref, buf_ref, acc_ref, sems):
    own = buf_ref.shape[0] - sel_ref.shape[0]
    me = lax.axis_index("z") * lax.axis_size("core") + lax.axis_index("core")
    copies = [pltpu.make_async_copy(group_ref.at[pl.ds(me * own, own)], buf_ref.at[pl.ds(0, own)], sems.at[0])]
    for q in range(sel_ref.shape[0]):
        copies.append(
            pltpu.make_async_copy(group_ref.at[sel_ref[q]], buf_ref.at[own + q], sems.at[q + 1])
        )
    for cp in copies:
        cp.start()
    out_ref[...] = jnp.zeros_like(out_ref)
    for cp in copies:
        cp.wait()
    spans = ((CG, 2 * CG),)
    accumulate_rows(rows, slots, spans, src_ref, live_ref, lcol_ref, pcol_ref, a_ref, buf_ref, pt_ref, out_ref, acc_ref)


def side_kernel(rows, slots, src_ref, live_ref, lcol_ref, pcol_ref, a_ref, lower_ref, upper_ref, pt_ref, prior_ref, out_ref, buf_ref, acc_ref, sems):
    half = lower_ref.shape[0]
    copies = [
        pltpu.make_async_copy(lower_ref, buf_ref.at[pl.ds(0, half)], sems.at[0]),
        pltpu.make_async_copy(upper_ref, buf_ref.at[pl.ds(half, half)], sems.at[1]),
    ]
    for cp in copies:
        cp.start()
    out_ref[...] = prior_ref[...]
    for cp in copies:
        cp.wait()
    spans = ((0, CG), (2 * CG, 3 * CG))
    accumulate_rows(rows, slots, spans, src_ref, live_ref, lcol_ref, pcol_ref, a_ref, buf_ref, pt_ref, out_ref, acc_ref)


def pick_kernel(up_sel, down_sel, group_ref, up_ref, down_ref, sems):
    count = up_sel.shape[0]
    copies = []
    for q in range(count):
        copies.append(pltpu.make_async_copy(group_ref.at[up_sel[q]], up_ref.at[q], sems.at[q]))
        copies.append(
            pltpu.make_async_copy(group_ref.at[down_sel[q]], down_ref.at[q], sems.at[count + q])
        )
    for cp in copies:
        cp.start()
    for cp in copies:
        cp.wait()


SMEM = pl.BlockSpec(memory_space=pltpu.SMEM)
VMEM = pl.BlockSpec(memory_space=pltpu.VMEM)
ANY = pl.BlockSpec(memory_space=pl.ANY)


def cost(a_tiles, width, extra_bytes):
    rows, slots, bs, _ = a_tiles.shape
    flops = 2 * rows * slots * 2 * bs ** 3 + 2 * rows * 2 * bs * bs * width * bs
    return pl.CostEstimate(
        flops=flops,
        bytes_accessed=a_tiles.size * 2 + extra_bytes + CG * bs * width * bs * 4,
        transcendentals=0,
    )


def middle_product(a_tiles, group_tiles, p_t, sel, src, live, lcol, pcol):
    rows, slots, bs, _ = a_tiles.shape
    count = sel.shape[0]
    width = 3 * CG
    return pl.pallas_call(
        functools.partial(middle_kernel, rows, slots),
        out_shape=jax.ShapeDtypeStruct((CG, bs, width * bs), jnp.float32),
        in_specs=[SMEM, SMEM, SMEM, SMEM, SMEM, VMEM, ANY, VMEM],
        out_specs=VMEM,
        scratch_shapes=[
            pltpu.VMEM((rows + count, 2, bs, bs), jnp.bfloat16),
            pltpu.VMEM((bs, width * bs), jnp.float32),
            pltpu.SemaphoreType.DMA((count + 1,)),
        ],
        compiler_params=pltpu.CompilerParams(vmem_limit_bytes=VMEM_LIMIT),
        cost_estimate=cost(a_tiles, width, (rows + count) * 2 * bs * bs * 2),
    )(src, live, lcol, pcol, sel, a_tiles, group_tiles, p_t)


def side_product(a_tiles, lower, upper, p_t, src, live, lcol, pcol, prior):
    rows, slots, bs, _ = a_tiles.shape
    count = lower.shape[0]
    width = 3 * CG
    return pl.pallas_call(
        functools.partial(side_kernel, rows, slots),
        out_shape=jax.ShapeDtypeStruct((CG, bs, width * bs), jnp.float32),
        in_specs=[SMEM, SMEM, SMEM, SMEM, VMEM, ANY, ANY, VMEM, VMEM],
        input_output_aliases={8: 0},
        out_specs=VMEM,
        scratch_shapes=[
            pltpu.VMEM((2 * count, 2, bs, bs), jnp.bfloat16),
            pltpu.VMEM((bs, width * bs), jnp.float32),
            pltpu.SemaphoreType.DMA((2,)),
        ],
        compiler_params=pltpu.CompilerParams(vmem_limit_bytes=VMEM_LIMIT),
        cost_estimate=cost(a_tiles, width, 2 * count * 2 * bs * bs * 2),
    )(src, live, lcol, pcol, a_tiles, lower, upper, p_t, prior)


def pick_rows(group_tiles, up_sel, down_sel):
    count = up_sel.shape[0]
    shape = (count,) + group_tiles.shape[1:]
    out = jax.ShapeDtypeStruct(shape, group_tiles.dtype)
    nbytes = 2 * 2 * count * group_tiles[0].size * 2
    return pl.pallas_call(
        pick_kernel,
        out_shape=(out, out),
        in_specs=[SMEM, SMEM, ANY],
        out_specs=(VMEM, VMEM),
        scratch_shapes=[pltpu.SemaphoreType.DMA((2 * count,))],
        compiler_params=pltpu.CompilerParams(vmem_limit_bytes=VMEM_LIMIT),
        cost_estimate=pl.CostEstimate(flops=0, bytes_accessed=nbytes, transcendentals=0),
    )(up_sel, down_sel, group_tiles)


def body(a_tiles, a_cols, p_tiles, p_cols, send_list):
    z_count = lax.axis_size("z")
    core_count = lax.axis_size("core")
    col_count = z_count * core_count
    row_count = lax.axis_size("row")
    g = lax.axis_index("row")
    c = lax.axis_index("z") * core_count + lax.axis_index("core")
    own_rows, slot_count = a_cols.shape
    tile_count = p_cols.shape[1]
    block_size = a_tiles.shape[-1]

    ints = jnp.concatenate([p_cols.reshape(-1), send_list.reshape(-1)])
    group_ints = lax.all_gather(ints, ("z", "core"))
    group_pcols = group_ints[:, : own_rows * tile_count].reshape(-1, tile_count)
    group_send = group_ints[:, own_rows * tile_count :]
    group_tiles = lax.all_gather(p_tiles, ("z", "core"), tiled=True)

    q = jnp.arange(col_count, dtype=jnp.int32)
    base = q * own_rows

    def selection(t):
        return base + jnp.clip(group_send[:, 3 * c + t], 0, own_rows - 1)

    up_sel, mid_sel, down_sel = selection(0), selection(1), selection(2)
    up_tiles, down_tiles = pick_rows(group_tiles, up_sel, down_sel)

    def cols_of(t):
        return group_pcols[q * own_rows + jnp.clip(group_send[:, 3 * c + t], 0, own_rows - 1)]

    lower_tiles, lower_cols = from_behind((up_tiles, cols_of(0)), "row", 1)
    upper_tiles, upper_cols = from_behind((down_tiles, cols_of(2)), "row", -1)
    mid_cols = cols_of(1)

    b = a_cols.reshape(-1)
    live = b >= 0
    bb = jnp.clip(b, 0, own_rows + 3 * col_count - 1)
    is_own = bb < own_rows
    ghost = jnp.maximum(bb - own_rows, 0)
    ghost_q = ghost // 3
    stream = ghost % 3
    src_group = g + stream - 1
    in_range = (src_group >= 0) & (src_group < row_count)
    pcol = jnp.clip(p_cols, 0, CG - 1)

    mid_src = jnp.where(is_own, bb, own_rows + ghost_q)
    mid_live = (live & (is_own | (stream == 1))).astype(jnp.int32)
    mid_table = jnp.concatenate([pcol, jnp.clip(mid_cols, 0, CG - 1)], axis=0) + CG
    mid_lcol = mid_table[mid_src].reshape(-1)

    side_src = jnp.where(stream == 0, ghost_q, col_count + ghost_q)
    side_live = (live & ~is_own & (stream != 1) & in_range).astype(jnp.int32)
    side_table = jnp.concatenate(
        [jnp.clip(lower_cols, 0, CG - 1), jnp.clip(upper_cols, 0, CG - 1) + 2 * CG], axis=0
    )
    side_lcol = side_table[side_src].reshape(-1)

    p_t = jnp.swapaxes(p_tiles, -1, -2)
    pcol = pcol.reshape(-1)
    mid = middle_product(a_tiles, group_tiles, p_t, mid_sel, mid_src, mid_live, mid_lcol, pcol)
    partial = side_product(
        a_tiles, lower_tiles, upper_tiles, p_t, side_src, side_live, side_lcol, pcol, mid
    )
    partial = partial.reshape(CG * block_size, 3 * CG * block_size)
    partial = lax.psum_scatter(partial, "z", scatter_dimension=0, tiled=True)
    k = lax.axis_index("core")
    half = partial.shape[0] // 2
    mine = lax.dynamic_slice_in_dim(partial, k * half, half, axis=0)
    other = lax.dynamic_slice_in_dim(partial, (1 - k) * half, half, axis=0)
    return mine + lax.ppermute(other, "core", [(0, 1), (1, 0)])


def solution(mesh):
    rows, cols = mesh.devices.shape
    chip_mesh = jax.sharding.Mesh(mesh.devices.reshape(rows, cols // 2, 2), ("row", "z", "core"))
    split = ("row", "z", "core")
    in_specs = (
        P(split, None, None, None),
        P(split, None),
        P(split, None, None, None),
        P(split, None),
        P(split, None),
    )
    out_specs = P(split, None)
    return jax.shard_map(body, mesh=chip_mesh, in_specs=in_specs, out_specs=out_specs, check_vma=False)
```

```python
import functools

import jax
import jax.numpy as jnp
from jax import lax
from jax.experimental import pallas as pl
from jax.experimental.pallas import tpu as pltpu
from jax.sharding import PartitionSpec as P

CG = 4
VMEM_LIMIT = 60 * 1024 * 1024


def from_behind(value, axis, steps):
    count = lax.axis_size(axis)
    leading, last = (max(0, -steps), min(count, count - steps))
    return lax.ppermute(value, axis, [(source, source + steps) for source in range(leading, last)])


def accumulate_rows(rows, slots, spans, src_ref, live_ref, lcol_ref, pcol_ref, a_ref, b_ref, pt_ref, out_ref, acc_ref):
    bs = a_ref.shape[-1]
    for i in range(rows):
        for lo, hi in spans:
            acc_ref[:, lo * bs : hi * bs] = jnp.zeros((bs, (hi - lo) * bs), jnp.float32)

        def slot(k, carry):
            s = i * slots + k

            @pl.when(live_ref[s] != 0)
            def _():
                src = src_ref[s]
                a = a_ref[i, k]
                for p in range(2):
                    col = pl.multiple_of(lcol_ref[2 * s + p] * bs, bs)
                    acc_ref[:, pl.ds(col, bs)] += jnp.dot(
                        a, b_ref[p][src], preferred_element_type=jnp.float32
                    )

            return carry

        lax.fori_loop(0, slots, slot, 0)
        for lo, hi in spans:
            prod = acc_ref[:, lo * bs : hi * bs].astype(jnp.bfloat16)
            for p in range(2):
                m = pcol_ref[2 * i + p]
                out_ref[m, :, lo * bs : hi * bs] += jnp.dot(
                    pt_ref[i, p], prod, preferred_element_type=jnp.float32
                )


def middle_kernel(rows, slots, src_ref, live_ref, lcol_ref, pcol_ref, sel_ref, a_ref, group0_ref, group1_ref, pt_ref, out_ref, buf0_ref, buf1_ref, acc_ref, sems):
    count = sel_ref.shape[0]
    own = buf0_ref.shape[0] - count
    me = lax.axis_index("z") * lax.axis_size("core") + lax.axis_index("core")
    copies = []
    for p, (group_ref, buf_ref) in enumerate(((group0_ref, buf0_ref), (group1_ref, buf1_ref))):
        base = p * (count + 1)
        copies.append(
            pltpu.make_async_copy(group_ref.at[pl.ds(me * own, own)], buf_ref.at[pl.ds(0, own)], sems.at[base])
        )
        for q in range(count):
            copies.append(
                pltpu.make_async_copy(group_ref.at[sel_ref[q]], buf_ref.at[own + q], sems.at[base + q + 1])
            )
    buf_ref = (buf0_ref, buf1_ref)
    for cp in copies:
        cp.start()
    out_ref[...] = jnp.zeros_like(out_ref)
    for cp in copies:
        cp.wait()
    spans = ((CG, 2 * CG),)
    accumulate_rows(rows, slots, spans, src_ref, live_ref, lcol_ref, pcol_ref, a_ref, buf_ref, pt_ref, out_ref, acc_ref)


def side_kernel(rows, slots, src_ref, live_ref, lcol_ref, pcol_ref, a_ref, lower0_ref, lower1_ref, upper0_ref, upper1_ref, pt_ref, prior_ref, out_ref, buf0_ref, buf1_ref, acc_ref, sems):
    half = lower0_ref.shape[0]
    copies = [
        pltpu.make_async_copy(lower0_ref, buf0_ref.at[pl.ds(0, half)], sems.at[0]),
        pltpu.make_async_copy(upper0_ref, buf0_ref.at[pl.ds(half, half)], sems.at[1]),
        pltpu.make_async_copy(lower1_ref, buf1_ref.at[pl.ds(0, half)], sems.at[2]),
        pltpu.make_async_copy(upper1_ref, buf1_ref.at[pl.ds(half, half)], sems.at[3]),
    ]
    buf_ref = (buf0_ref, buf1_ref)
    for cp in copies:
        cp.start()
    out_ref[...] = prior_ref[...]
    for cp in copies:
        cp.wait()
    spans = ((0, CG), (2 * CG, 3 * CG))
    accumulate_rows(rows, slots, spans, src_ref, live_ref, lcol_ref, pcol_ref, a_ref, buf_ref, pt_ref, out_ref, acc_ref)


def pick_kernel(up_sel, down_sel, group_ref, up_ref, down_ref, sems):
    count = up_sel.shape[0]
    copies = []
    for q in range(count):
        copies.append(pltpu.make_async_copy(group_ref.at[up_sel[q]], up_ref.at[q], sems.at[q]))
        copies.append(
            pltpu.make_async_copy(group_ref.at[down_sel[q]], down_ref.at[q], sems.at[count + q])
        )
    for cp in copies:
        cp.start()
    for cp in copies:
        cp.wait()


SMEM = pl.BlockSpec(memory_space=pltpu.SMEM)
VMEM = pl.BlockSpec(memory_space=pltpu.VMEM)
ANY = pl.BlockSpec(memory_space=pl.ANY)


def cost(a_tiles, width, extra_bytes):
    rows, slots, bs, _ = a_tiles.shape
    flops = 2 * rows * slots * 2 * bs ** 3 + 2 * rows * 2 * bs * bs * width * bs
    return pl.CostEstimate(
        flops=flops,
        bytes_accessed=a_tiles.size * 2 + extra_bytes + CG * bs * width * bs * 4,
        transcendentals=0,
    )


def middle_product(a_tiles, group0, group1, p_t, sel, src, live, lcol, pcol):
    rows, slots, bs, _ = a_tiles.shape
    count = sel.shape[0]
    width = 3 * CG
    return pl.pallas_call(
        functools.partial(middle_kernel, rows, slots),
        out_shape=jax.ShapeDtypeStruct((CG, bs, width * bs), jnp.float32),
        in_specs=[SMEM, SMEM, SMEM, SMEM, SMEM, VMEM, ANY, ANY, VMEM],
        out_specs=VMEM,
        scratch_shapes=[
            pltpu.VMEM((rows + count, bs, bs), jnp.bfloat16),
            pltpu.VMEM((rows + count, bs, bs), jnp.bfloat16),
            pltpu.VMEM((bs, width * bs), jnp.float32),
            pltpu.SemaphoreType.DMA((2 * (count + 1),)),
        ],
        compiler_params=pltpu.CompilerParams(vmem_limit_bytes=VMEM_LIMIT),
        cost_estimate=cost(a_tiles, width, (rows + count) * 2 * bs * bs * 2),
    )(src, live, lcol, pcol, sel, a_tiles, group0, group1, p_t)


def side_product(a_tiles, lower0, lower1, upper0, upper1, p_t, src, live, lcol, pcol, prior):
    rows, slots, bs, _ = a_tiles.shape
    count = lower0.shape[0]
    width = 3 * CG
    return pl.pallas_call(
        functools.partial(side_kernel, rows, slots),
        out_shape=jax.ShapeDtypeStruct((CG, bs, width * bs), jnp.float32),
        in_specs=[SMEM, SMEM, SMEM, SMEM, VMEM, ANY, ANY, ANY, ANY, VMEM, VMEM],
        input_output_aliases={10: 0},
        out_specs=VMEM,
        scratch_shapes=[
            pltpu.VMEM((2 * count, bs, bs), jnp.bfloat16),
            pltpu.VMEM((2 * count, bs, bs), jnp.bfloat16),
            pltpu.VMEM((bs, width * bs), jnp.float32),
            pltpu.SemaphoreType.DMA((4,)),
        ],
        compiler_params=pltpu.CompilerParams(vmem_limit_bytes=VMEM_LIMIT),
        cost_estimate=cost(a_tiles, width, 2 * count * 2 * bs * bs * 2),
    )(src, live, lcol, pcol, a_tiles, lower0, lower1, upper0, upper1, p_t, prior)


def pick_rows(group_tiles, up_sel, down_sel):
    count = up_sel.shape[0]
    shape = (count,) + group_tiles.shape[1:]
    out = jax.ShapeDtypeStruct(shape, group_tiles.dtype)
    nbytes = 2 * 2 * count * group_tiles[0].size
    return pl.pallas_call(
        pick_kernel,
        out_shape=(out, out),
        in_specs=[SMEM, SMEM, ANY],
        out_specs=(VMEM, VMEM),
        scratch_shapes=[pltpu.SemaphoreType.DMA((2 * count,))],
        compiler_params=pltpu.CompilerParams(vmem_limit_bytes=VMEM_LIMIT),
        cost_estimate=pl.CostEstimate(flops=0, bytes_accessed=nbytes, transcendentals=0),
    )(up_sel, down_sel, group_tiles)


def body(a_tiles, a_cols, p_tiles, p_cols, send_list):
    z_count = lax.axis_size("z")
    core_count = lax.axis_size("core")
    col_count = z_count * core_count
    row_count = lax.axis_size("row")
    g = lax.axis_index("row")
    c = lax.axis_index("z") * core_count + lax.axis_index("core")
    own_rows, slot_count = a_cols.shape
    tile_count = p_cols.shape[1]
    block_size = a_tiles.shape[-1]

    ints = jnp.concatenate([p_cols.reshape(-1), send_list.reshape(-1)])
    group_ints = lax.all_gather(ints, ("z", "core"))
    group_pcols = group_ints[:, : own_rows * tile_count].reshape(-1, tile_count)
    group_send = group_ints[:, own_rows * tile_count :]
    group0 = lax.all_gather(p_tiles[:, 0], ("z", "core"), tiled=True)

    q = jnp.arange(col_count, dtype=jnp.int32)
    base = q * own_rows

    def selection(t):
        return base + jnp.clip(group_send[:, 3 * c + t], 0, own_rows - 1)

    up_sel, mid_sel, down_sel = selection(0), selection(1), selection(2)
    up0, down0 = pick_rows(group0, up_sel, down_sel)
    second, up0, down0 = lax.optimization_barrier((p_tiles[:, 1], up0, down0))
    lower0, upper0 = from_behind(up0, "row", 1), from_behind(down0, "row", -1)
    group1 = lax.all_gather(second, ("z", "core"), tiled=True)
    up1, down1 = pick_rows(group1, up_sel, down_sel)
    lower1, upper1 = from_behind(up1, "row", 1), from_behind(down1, "row", -1)

    def cols_of(t):
        return group_pcols[q * own_rows + jnp.clip(group_send[:, 3 * c + t], 0, own_rows - 1)]

    lower_cols = from_behind(cols_of(0), "row", 1)
    upper_cols = from_behind(cols_of(2), "row", -1)
    mid_cols = cols_of(1)

    b = a_cols.reshape(-1)
    live = b >= 0
    bb = jnp.clip(b, 0, own_rows + 3 * col_count - 1)
    is_own = bb < own_rows
    ghost = jnp.maximum(bb - own_rows, 0)
    ghost_q = ghost // 3
    stream = ghost % 3
    src_group = g + stream - 1
    in_range = (src_group >= 0) & (src_group < row_count)
    pcol = jnp.clip(p_cols, 0, CG - 1)

    mid_src = jnp.where(is_own, bb, own_rows + ghost_q)
    mid_live = (live & (is_own | (stream == 1))).astype(jnp.int32)
    mid_table = jnp.concatenate([pcol, jnp.clip(mid_cols, 0, CG - 1)], axis=0) + CG
    mid_lcol = mid_table[mid_src].reshape(-1)

    side_src = jnp.where(stream == 0, ghost_q, col_count + ghost_q)
    side_live = (live & ~is_own & (stream != 1) & in_range).astype(jnp.int32)
    side_table = jnp.concatenate(
        [jnp.clip(lower_cols, 0, CG - 1), jnp.clip(upper_cols, 0, CG - 1) + 2 * CG], axis=0
    )
    side_lcol = side_table[side_src].reshape(-1)

    p_t = jnp.swapaxes(p_tiles, -1, -2)
    pcol = pcol.reshape(-1)
    mid = middle_product(a_tiles, group0, group1, p_t, mid_sel, mid_src, mid_live, mid_lcol, pcol)
    partial = side_product(
        a_tiles, lower0, lower1, upper0, upper1, p_t, side_src, side_live, side_lcol, pcol, mid
    )
    partial = partial.reshape(CG * block_size, 3 * CG * block_size)
    partial = lax.psum_scatter(partial, "z", scatter_dimension=0, tiled=True)
    k = lax.axis_index("core")
    half = partial.shape[0] // 2
    mine = lax.dynamic_slice_in_dim(partial, k * half, half, axis=0)
    other = lax.dynamic_slice_in_dim(partial, (1 - k) * half, half, axis=0)
    return mine + lax.ppermute(other, "core", [(0, 1), (1, 0)])


def solution(mesh):
    rows, cols = mesh.devices.shape
    chip_mesh = jax.sharding.Mesh(mesh.devices.reshape(rows, cols // 2, 2), ("row", "z", "core"))
    split = ("row", "z", "core")
    in_specs = (
        P(split, None, None, None),
        P(split, None),
        P(split, None, None, None),
        P(split, None),
        P(split, None),
    )
    out_specs = P(split, None)
    return jax.shard_map(body, mesh=chip_mesh, in_specs=in_specs, out_specs=out_specs, check_vma=False)
```

```python
import functools

import jax
import jax.numpy as jnp
from jax import lax
from jax.experimental import pallas as pl
from jax.experimental.pallas import tpu as pltpu
from jax.sharding import PartitionSpec as P

CG = 4
VMEM_LIMIT = 60 * 1024 * 1024


def from_behind(value, axis, steps):
    count = lax.axis_size(axis)
    leading, last = (max(0, -steps), min(count, count - steps))
    return lax.ppermute(value, axis, [(source, source + steps) for source in range(leading, last)])


def accumulate_rows(rows, slots, spans, src_ref, live_ref, lcol_ref, pcol_ref, a_ref, b_ref, pt_ref, out_ref, acc_ref):
    bs = a_ref.shape[-1]
    for i in range(rows):
        for lo, hi in spans:
            acc_ref[:, lo * bs : hi * bs] = jnp.zeros((bs, (hi - lo) * bs), jnp.float32)

        def slot(k, carry):
            s = i * slots + k

            @pl.when(live_ref[s] != 0)
            def _():
                src = src_ref[s]
                a = a_ref[i, k]
                for p in range(2):
                    col = pl.multiple_of(lcol_ref[2 * s + p] * bs, bs)
                    acc_ref[:, pl.ds(col, bs)] += jnp.dot(
                        a, b_ref[src, p], preferred_element_type=jnp.float32
                    )

            return carry

        lax.fori_loop(0, slots, slot, 0)
        for lo, hi in spans:
            prod = acc_ref[:, lo * bs : hi * bs].astype(jnp.bfloat16)
            for p in range(2):
                m = pcol_ref[2 * i + p]
                out_ref[m, :, lo * bs : hi * bs] += jnp.dot(
                    pt_ref[i, p], prod, preferred_element_type=jnp.float32
                )


def middle_kernel(rows, slots, src_ref, live_ref, lcol_ref, pcol_ref, sel_ref, a_ref, group_ref, pt_ref, out_ref, buf_ref, acc_ref, sems):
    own = buf_ref.shape[0] - sel_ref.shape[0]
    me = lax.axis_index("z") * lax.axis_size("core") + lax.axis_index("core")
    copies = [pltpu.make_async_copy(group_ref.at[pl.ds(me * own, own)], buf_ref.at[pl.ds(0, own)], sems.at[0])]
    for q in range(sel_ref.shape[0]):
        copies.append(
            pltpu.make_async_copy(group_ref.at[sel_ref[q]], buf_ref.at[own + q], sems.at[q + 1])
        )
    for cp in copies:
        cp.start()
    out_ref[...] = jnp.zeros_like(out_ref)
    for cp in copies:
        cp.wait()
    spans = ((CG, 2 * CG),)
    accumulate_rows(rows, slots, spans, src_ref, live_ref, lcol_ref, pcol_ref, a_ref, buf_ref, pt_ref, out_ref, acc_ref)


def side_kernel(rows, slots, src_ref, live_ref, lcol_ref, pcol_ref, a_ref, lower_ref, upper_ref, pt_ref, prior_ref, out_ref, buf_ref, acc_ref, sems):
    half = lower_ref.shape[0]
    copies = [
        pltpu.make_async_copy(lower_ref, buf_ref.at[pl.ds(0, half)], sems.at[0]),
        pltpu.make_async_copy(upper_ref, buf_ref.at[pl.ds(half, half)], sems.at[1]),
    ]
    for cp in copies:
        cp.start()
    out_ref[...] = prior_ref[...]
    for cp in copies:
        cp.wait()
    spans = ((0, CG), (2 * CG, 3 * CG))
    accumulate_rows(rows, slots, spans, src_ref, live_ref, lcol_ref, pcol_ref, a_ref, buf_ref, pt_ref, out_ref, acc_ref)


def pick_kernel(up_sel, down_sel, group_ref, up_ref, down_ref, sems):
    count = up_sel.shape[0]
    copies = []
    for q in range(count):
        copies.append(pltpu.make_async_copy(group_ref.at[up_sel[q]], up_ref.at[q], sems.at[q]))
        copies.append(
            pltpu.make_async_copy(group_ref.at[down_sel[q]], down_ref.at[q], sems.at[count + q])
        )
    for cp in copies:
        cp.start()
    for cp in copies:
        cp.wait()


SMEM = pl.BlockSpec(memory_space=pltpu.SMEM)
VMEM = pl.BlockSpec(memory_space=pltpu.VMEM)
ANY = pl.BlockSpec(memory_space=pl.ANY)


def cost(a_tiles, width, extra_bytes):
    rows, slots, bs, _ = a_tiles.shape
    flops = 2 * rows * slots * 2 * bs ** 3 + 2 * rows * 2 * bs * bs * width * bs
    return pl.CostEstimate(
        flops=flops,
        bytes_accessed=a_tiles.size * 2 + extra_bytes + CG * bs * width * bs * 4,
        transcendentals=0,
    )


def middle_product(a_tiles, group_tiles, p_t, sel, src, live, lcol, pcol):
    rows, slots, bs, _ = a_tiles.shape
    count = sel.shape[0]
    width = 3 * CG
    return pl.pallas_call(
        functools.partial(middle_kernel, rows, slots),
        out_shape=jax.ShapeDtypeStruct((CG, bs, width * bs), jnp.float32),
        in_specs=[SMEM, SMEM, SMEM, SMEM, SMEM, VMEM, ANY, VMEM],
        out_specs=VMEM,
        scratch_shapes=[
            pltpu.VMEM((rows + count, 2, bs, bs), jnp.bfloat16),
            pltpu.VMEM((bs, width * bs), jnp.float32),
            pltpu.SemaphoreType.DMA((count + 1,)),
        ],
        compiler_params=pltpu.CompilerParams(vmem_limit_bytes=VMEM_LIMIT),
        cost_estimate=cost(a_tiles, width, (rows + count) * 2 * bs * bs * 2),
    )(src, live, lcol, pcol, sel, a_tiles, group_tiles, p_t)


def side_product(a_tiles, lower, upper, p_t, src, live, lcol, pcol, prior):
    rows, slots, bs, _ = a_tiles.shape
    count = lower.shape[0]
    width = 3 * CG
    return pl.pallas_call(
        functools.partial(side_kernel, rows, slots),
        out_shape=jax.ShapeDtypeStruct((CG, bs, width * bs), jnp.float32),
        in_specs=[SMEM, SMEM, SMEM, SMEM, VMEM, ANY, ANY, VMEM, VMEM],
        input_output_aliases={8: 0},
        out_specs=VMEM,
        scratch_shapes=[
            pltpu.VMEM((2 * count, 2, bs, bs), jnp.bfloat16),
            pltpu.VMEM((bs, width * bs), jnp.float32),
            pltpu.SemaphoreType.DMA((2,)),
        ],
        compiler_params=pltpu.CompilerParams(vmem_limit_bytes=VMEM_LIMIT),
        cost_estimate=cost(a_tiles, width, 2 * count * 2 * bs * bs * 2),
    )(src, live, lcol, pcol, a_tiles, lower, upper, p_t, prior)


def pick_rows(group_tiles, up_sel, down_sel):
    count = up_sel.shape[0]
    shape = (count,) + group_tiles.shape[1:]
    out = jax.ShapeDtypeStruct(shape, group_tiles.dtype)
    nbytes = 2 * 2 * count * group_tiles[0].size * 2
    return pl.pallas_call(
        pick_kernel,
        out_shape=(out, out),
        in_specs=[SMEM, SMEM, ANY],
        out_specs=(VMEM, VMEM),
        scratch_shapes=[pltpu.SemaphoreType.DMA((2 * count,))],
        compiler_params=pltpu.CompilerParams(vmem_limit_bytes=VMEM_LIMIT),
        cost_estimate=pl.CostEstimate(flops=0, bytes_accessed=nbytes, transcendentals=0),
    )(up_sel, down_sel, group_tiles)


def body(a_tiles, a_cols, p_tiles, p_cols, send_list):
    z_count = lax.axis_size("z")
    core_count = lax.axis_size("core")
    col_count = z_count * core_count
    row_count = lax.axis_size("row")
    g = lax.axis_index("row")
    c = lax.axis_index("z") * core_count + lax.axis_index("core")
    own_rows, slot_count = a_cols.shape
    tile_count = p_cols.shape[1]
    block_size = a_tiles.shape[-1]

    ints = jnp.concatenate([p_cols.reshape(-1), send_list.reshape(-1)])
    group_ints = lax.all_gather(ints, ("z", "core"))
    group_pcols = group_ints[:, : own_rows * tile_count].reshape(-1, tile_count)
    group_send = group_ints[:, own_rows * tile_count :]
    group_tiles = lax.all_gather(p_tiles, ("z", "core"), tiled=True)

    q = jnp.arange(col_count, dtype=jnp.int32)
    base = q * own_rows

    def selection(t):
        return base + jnp.clip(group_send[:, 3 * c + t], 0, own_rows - 1)

    up_sel, mid_sel, down_sel = selection(0), selection(1), selection(2)
    up_tiles, down_tiles = pick_rows(group_tiles, up_sel, down_sel)

    def cols_of(t):
        return group_pcols[q * own_rows + jnp.clip(group_send[:, 3 * c + t], 0, own_rows - 1)]

    lower_tiles = from_behind(up_tiles, "row", 1)
    upper_tiles = from_behind(down_tiles, "row", -1)
    up_cols, down_cols, up_tiles = lax.optimization_barrier((cols_of(0), cols_of(2), up_tiles))
    lower_cols = from_behind(up_cols, "row", 1)
    upper_cols = from_behind(down_cols, "row", -1)
    mid_cols = cols_of(1)

    b = a_cols.reshape(-1)
    live = b >= 0
    bb = jnp.clip(b, 0, own_rows + 3 * col_count - 1)
    is_own = bb < own_rows
    ghost = jnp.maximum(bb - own_rows, 0)
    ghost_q = ghost // 3
    stream = ghost % 3
    src_group = g + stream - 1
    in_range = (src_group >= 0) & (src_group < row_count)
    pcol = jnp.clip(p_cols, 0, CG - 1)

    mid_src = jnp.where(is_own, bb, own_rows + ghost_q)
    mid_live = (live & (is_own | (stream == 1))).astype(jnp.int32)
    mid_table = jnp.concatenate([pcol, jnp.clip(mid_cols, 0, CG - 1)], axis=0) + CG
    mid_lcol = mid_table[mid_src].reshape(-1)

    side_src = jnp.where(stream == 0, ghost_q, col_count + ghost_q)
    side_live = (live & ~is_own & (stream != 1) & in_range).astype(jnp.int32)
    side_table = jnp.concatenate(
        [jnp.clip(lower_cols, 0, CG - 1), jnp.clip(upper_cols, 0, CG - 1) + 2 * CG], axis=0
    )
    side_lcol = side_table[side_src].reshape(-1)

    p_t = jnp.swapaxes(p_tiles, -1, -2)
    pcol = pcol.reshape(-1)
    mid = middle_product(a_tiles, group_tiles, p_t, mid_sel, mid_src, mid_live, mid_lcol, pcol)
    partial = side_product(
        a_tiles, lower_tiles, upper_tiles, p_t, side_src, side_live, side_lcol, pcol, mid
    )
    partial = partial.reshape(CG * block_size, 3 * CG * block_size)
    partial = lax.psum_scatter(partial, "z", scatter_dimension=0, tiled=True)
    k = lax.axis_index("core")
    half = partial.shape[0] // 2
    mine = lax.dynamic_slice_in_dim(partial, k * half, half, axis=0)
    other = lax.dynamic_slice_in_dim(partial, (1 - k) * half, half, axis=0)
    return mine + lax.ppermute(other, "core", [(0, 1), (1, 0)])


def solution(mesh):
    rows, cols = mesh.devices.shape
    chip_mesh = jax.sharding.Mesh(mesh.devices.reshape(rows, cols // 2, 2), ("row", "z", "core"))
    split = ("row", "z", "core")
    in_specs = (
        P(split, None, None, None),
        P(split, None),
        P(split, None, None, None),
        P(split, None),
        P(split, None),
    )
    out_specs = P(split, None)
    return jax.shard_map(body, mesh=chip_mesh, in_specs=in_specs, out_specs=out_specs, check_vma=False)
```

```python
import functools

import jax
import jax.numpy as jnp
from jax import lax
from jax.experimental import pallas as pl
from jax.experimental.pallas import tpu as pltpu
from jax.sharding import PartitionSpec as P

CG = 4
VMEM_LIMIT = 60 * 1024 * 1024


def from_behind(value, axis, steps):
    count = lax.axis_size(axis)
    leading, last = (max(0, -steps), min(count, count - steps))
    return lax.ppermute(value, axis, [(source, source + steps) for source in range(leading, last)])


def accumulate_rows(rows, slots, spans, src_ref, live_ref, lcol_ref, pcol_ref, a_ref, b_ref, pt_ref, out_ref, acc_ref):
    bs = a_ref.shape[-1]
    for i in range(rows):
        for lo, hi in spans:
            acc_ref[:, lo * bs : hi * bs] = jnp.zeros((bs, (hi - lo) * bs), jnp.float32)

        def slot(k, carry):
            s = i * slots + k

            @pl.when(live_ref[s] != 0)
            def _():
                src = src_ref[s]
                a = a_ref[i, k]
                for p in range(2):
                    col = pl.multiple_of(lcol_ref[2 * s + p] * bs, bs)
                    acc_ref[:, pl.ds(col, bs)] += jnp.dot(
                        a, b_ref[src, p], preferred_element_type=jnp.float32
                    )

            return carry

        lax.fori_loop(0, slots, slot, 0)
        for lo, hi in spans:
            prod = acc_ref[:, lo * bs : hi * bs].astype(jnp.bfloat16)
            for p in range(2):
                m = pcol_ref[2 * i + p]
                out_ref[m, :, lo * bs : hi * bs] += jnp.dot(
                    pt_ref[i, p], prod, preferred_element_type=jnp.float32
                )


def middle_kernel(rows, slots, src_ref, live_ref, lcol_ref, pcol_ref, sel_ref, a_ref, group_ref, pt_ref, out_ref, buf_ref, acc_ref, sems):
    own = buf_ref.shape[0] - sel_ref.shape[0]
    me = lax.axis_index("z") * lax.axis_size("core") + lax.axis_index("core")
    copies = [pltpu.make_async_copy(group_ref.at[pl.ds(me * own, own)], buf_ref.at[pl.ds(0, own)], sems.at[0])]
    for q in range(sel_ref.shape[0]):
        copies.append(
            pltpu.make_async_copy(group_ref.at[sel_ref[q]], buf_ref.at[own + q], sems.at[q + 1])
        )
    for cp in copies:
        cp.start()
    out_ref[...] = jnp.zeros_like(out_ref)
    for cp in copies:
        cp.wait()
    spans = ((CG, 2 * CG),)
    accumulate_rows(rows, slots, spans, src_ref, live_ref, lcol_ref, pcol_ref, a_ref, buf_ref, pt_ref, out_ref, acc_ref)


def side_kernel(rows, slots, src_ref, live_ref, lcol_ref, pcol_ref, a_ref, lower_ref, upper_ref, pt_ref, prior_ref, out_ref, buf_ref, acc_ref, sems):
    half = lower_ref.shape[0]
    copies = [
        pltpu.make_async_copy(prior_ref, out_ref, sems.at[2]),
        pltpu.make_async_copy(lower_ref, buf_ref.at[pl.ds(0, half)], sems.at[0]),
        pltpu.make_async_copy(upper_ref, buf_ref.at[pl.ds(half, half)], sems.at[1]),
    ]
    for cp in copies:
        cp.start()
    for cp in copies:
        cp.wait()
    spans = ((0, CG), (2 * CG, 3 * CG))
    accumulate_rows(rows, slots, spans, src_ref, live_ref, lcol_ref, pcol_ref, a_ref, buf_ref, pt_ref, out_ref, acc_ref)


def pick_kernel(up_sel, down_sel, group_ref, up_ref, down_ref, sems):
    count = up_sel.shape[0]
    copies = []
    for q in range(count):
        copies.append(pltpu.make_async_copy(group_ref.at[up_sel[q]], up_ref.at[q], sems.at[q]))
        copies.append(
            pltpu.make_async_copy(group_ref.at[down_sel[q]], down_ref.at[q], sems.at[count + q])
        )
    for cp in copies:
        cp.start()
    for cp in copies:
        cp.wait()


SMEM = pl.BlockSpec(memory_space=pltpu.SMEM)
VMEM = pl.BlockSpec(memory_space=pltpu.VMEM)
ANY = pl.BlockSpec(memory_space=pl.ANY)


def cost(a_tiles, width, extra_bytes):
    rows, slots, bs, _ = a_tiles.shape
    flops = 2 * rows * slots * 2 * bs ** 3 + 2 * rows * 2 * bs * bs * width * bs
    return pl.CostEstimate(
        flops=flops,
        bytes_accessed=a_tiles.size * 2 + extra_bytes + CG * bs * width * bs * 4,
        transcendentals=0,
    )


def middle_product(a_tiles, group_tiles, p_t, sel, src, live, lcol, pcol):
    rows, slots, bs, _ = a_tiles.shape
    count = sel.shape[0]
    width = 3 * CG
    return pl.pallas_call(
        functools.partial(middle_kernel, rows, slots),
        out_shape=jax.ShapeDtypeStruct((CG, bs, width * bs), jnp.float32),
        in_specs=[SMEM, SMEM, SMEM, SMEM, SMEM, VMEM, ANY, VMEM],
        out_specs=VMEM,
        scratch_shapes=[
            pltpu.VMEM((rows + count, 2, bs, bs), jnp.bfloat16),
            pltpu.VMEM((bs, width * bs), jnp.float32),
            pltpu.SemaphoreType.DMA((count + 1,)),
        ],
        compiler_params=pltpu.CompilerParams(vmem_limit_bytes=VMEM_LIMIT),
        cost_estimate=cost(a_tiles, width, (rows + count) * 2 * bs * bs * 2),
    )(src, live, lcol, pcol, sel, a_tiles, group_tiles, p_t)


def side_product(a_tiles, lower, upper, p_t, src, live, lcol, pcol, prior):
    rows, slots, bs, _ = a_tiles.shape
    count = lower.shape[0]
    width = 3 * CG
    return pl.pallas_call(
        functools.partial(side_kernel, rows, slots),
        out_shape=jax.ShapeDtypeStruct((CG, bs, width * bs), jnp.float32),
        in_specs=[SMEM, SMEM, SMEM, SMEM, VMEM, ANY, ANY, VMEM, ANY],
        input_output_aliases={8: 0},
        out_specs=VMEM,
        scratch_shapes=[
            pltpu.VMEM((2 * count, 2, bs, bs), jnp.bfloat16),
            pltpu.VMEM((bs, width * bs), jnp.float32),
            pltpu.SemaphoreType.DMA((3,)),
        ],
        compiler_params=pltpu.CompilerParams(vmem_limit_bytes=VMEM_LIMIT),
        cost_estimate=cost(a_tiles, width, 2 * count * 2 * bs * bs * 2),
    )(src, live, lcol, pcol, a_tiles, lower, upper, p_t, prior)


def pick_rows(group_tiles, up_sel, down_sel):
    count = up_sel.shape[0]
    shape = (count,) + group_tiles.shape[1:]
    out = jax.ShapeDtypeStruct(shape, group_tiles.dtype)
    nbytes = 2 * 2 * count * group_tiles[0].size * 2
    return pl.pallas_call(
        pick_kernel,
        out_shape=(out, out),
        in_specs=[SMEM, SMEM, ANY],
        out_specs=(ANY, ANY),
        scratch_shapes=[pltpu.SemaphoreType.DMA((2 * count,))],
        compiler_params=pltpu.CompilerParams(vmem_limit_bytes=VMEM_LIMIT),
        cost_estimate=pl.CostEstimate(flops=0, bytes_accessed=nbytes, transcendentals=0),
    )(up_sel, down_sel, group_tiles)


def body(a_tiles, a_cols, p_tiles, p_cols, send_list):
    z_count = lax.axis_size("z")
    core_count = lax.axis_size("core")
    col_count = z_count * core_count
    row_count = lax.axis_size("row")
    g = lax.axis_index("row")
    c = lax.axis_index("z") * core_count + lax.axis_index("core")
    own_rows, slot_count = a_cols.shape
    tile_count = p_cols.shape[1]
    block_size = a_tiles.shape[-1]

    ints = jnp.concatenate([p_cols.reshape(-1), send_list.reshape(-1)])
    group_ints = lax.all_gather(ints, ("z", "core"))
    group_pcols = group_ints[:, : own_rows * tile_count].reshape(-1, tile_count)
    group_send = group_ints[:, own_rows * tile_count :]
    group_tiles = lax.all_gather(p_tiles, ("z", "core"), tiled=True)

    q = jnp.arange(col_count, dtype=jnp.int32)
    base = q * own_rows

    def selection(t):
        return base + jnp.clip(group_send[:, 3 * c + t], 0, own_rows - 1)

    up_sel, mid_sel, down_sel = selection(0), selection(1), selection(2)
    up_tiles, down_tiles = pick_rows(group_tiles, up_sel, down_sel)

    def cols_of(t):
        return group_pcols[q * own_rows + jnp.clip(group_send[:, 3 * c + t], 0, own_rows - 1)]

    lower_tiles = from_behind(up_tiles, "row", 1)
    upper_tiles = from_behind(down_tiles, "row", -1)
    up_cols, down_cols, up_tiles = lax.optimization_barrier((cols_of(0), cols_of(2), up_tiles))
    lower_cols = from_behind(up_cols, "row", 1)
    upper_cols = from_behind(down_cols, "row", -1)
    mid_cols = cols_of(1)

    b = a_cols.reshape(-1)
    live = b >= 0
    bb = jnp.clip(b, 0, own_rows + 3 * col_count - 1)
    is_own = bb < own_rows
    ghost = jnp.maximum(bb - own_rows, 0)
    ghost_q = ghost // 3
    stream = ghost % 3
    src_group = g + stream - 1
    in_range = (src_group >= 0) & (src_group < row_count)
    pcol = jnp.clip(p_cols, 0, CG - 1)

    mid_src = jnp.where(is_own, bb, own_rows + ghost_q)
    mid_live = (live & (is_own | (stream == 1))).astype(jnp.int32)
    mid_table = jnp.concatenate([pcol, jnp.clip(mid_cols, 0, CG - 1)], axis=0) + CG
    mid_lcol = mid_table[mid_src].reshape(-1)

    side_src = jnp.where(stream == 0, ghost_q, col_count + ghost_q)
    side_live = (live & ~is_own & (stream != 1) & in_range).astype(jnp.int32)
    side_table = jnp.concatenate(
        [jnp.clip(lower_cols, 0, CG - 1), jnp.clip(upper_cols, 0, CG - 1) + 2 * CG], axis=0
    )
    side_lcol = side_table[side_src].reshape(-1)

    p_t = jnp.swapaxes(p_tiles, -1, -2)
    pcol = pcol.reshape(-1)
    mid = middle_product(a_tiles, group_tiles, p_t, mid_sel, mid_src, mid_live, mid_lcol, pcol)
    partial = side_product(
        a_tiles, lower_tiles, upper_tiles, p_t, side_src, side_live, side_lcol, pcol, mid
    )
    partial = partial.reshape(CG * block_size, 3 * CG * block_size)
    partial = lax.psum_scatter(partial, "z", scatter_dimension=0, tiled=True)
    k = lax.axis_index("core")
    half = partial.shape[0] // 2
    mine = lax.dynamic_slice_in_dim(partial, k * half, half, axis=0)
    other = lax.dynamic_slice_in_dim(partial, (1 - k) * half, half, axis=0)
    return mine + lax.ppermute(other, "core", [(0, 1), (1, 0)])


def solution(mesh):
    rows, cols = mesh.devices.shape
    chip_mesh = jax.sharding.Mesh(mesh.devices.reshape(rows, cols // 2, 2), ("row", "z", "core"))
    split = ("row", "z", "core")
    in_specs = (
        P(split, None, None, None),
        P(split, None),
        P(split, None, None, None),
        P(split, None),
        P(split, None),
    )
    out_specs = P(split, None)
    return jax.shard_map(body, mesh=chip_mesh, in_specs=in_specs, out_specs=out_specs, check_vma=False)
```

```python
import functools

import jax
import jax.numpy as jnp
from jax import lax
from jax.experimental import pallas as pl
from jax.experimental.pallas import tpu as pltpu
from jax.sharding import PartitionSpec as P

CG = 4
VMEM_LIMIT = 60 * 1024 * 1024


def from_behind(value, axis, steps):
    count = lax.axis_size(axis)
    leading, last = (max(0, -steps), min(count, count - steps))
    return lax.ppermute(value, axis, [(source, source + steps) for source in range(leading, last)])


def accumulate_rows(rows, slots, spans, src_ref, live_ref, lcol_ref, pcol_ref, a_ref, b_ref, pt_ref, out_ref, acc_ref):
    bs = a_ref.shape[-1]
    for i in range(rows):
        for lo, hi in spans:
            acc_ref[:, lo * bs : hi * bs] = jnp.zeros((bs, (hi - lo) * bs), jnp.float32)

        def slot(k, carry):
            s = i * slots + k

            @pl.when(live_ref[s] != 0)
            def _():
                src = src_ref[s]
                both = jnp.dot(a_ref[i, k], b_ref[src], preferred_element_type=jnp.float32)
                for p in range(2):
                    col = pl.multiple_of(lcol_ref[2 * s + p] * bs, bs)
                    acc_ref[:, pl.ds(col, bs)] += both[:, p * bs : (p + 1) * bs]

            return carry

        lax.fori_loop(0, slots, slot, 0)
        for lo, hi in spans:
            prod = acc_ref[:, lo * bs : hi * bs].astype(jnp.bfloat16)
            for p in range(2):
                m = pcol_ref[2 * i + p]
                out_ref[m, :, lo * bs : hi * bs] += jnp.dot(
                    pt_ref[i, p], prod, preferred_element_type=jnp.float32
                )


def middle_kernel(rows, slots, src_ref, live_ref, lcol_ref, pcol_ref, sel_ref, a_ref, group_ref, pt_ref, out_ref, buf_ref, acc_ref, sems):
    count = sel_ref.shape[0]
    own = buf_ref.shape[0] - count
    bs = group_ref.shape[-1]
    me = lax.axis_index("z") * lax.axis_size("core") + lax.axis_index("core")
    copies = []
    for p in range(2):
        base = p * (count + 1)
        lanes = pl.ds(p * bs, bs)
        copies.append(
            pltpu.make_async_copy(group_ref.at[pl.ds(me * own, own), p], buf_ref.at[pl.ds(0, own), :, lanes], sems.at[base])
        )
        for q in range(count):
            copies.append(
                pltpu.make_async_copy(group_ref.at[sel_ref[q], p], buf_ref.at[own + q, :, lanes], sems.at[base + q + 1])
            )
    for cp in copies:
        cp.start()
    out_ref[...] = jnp.zeros_like(out_ref)
    for cp in copies:
        cp.wait()
    spans = ((CG, 2 * CG),)
    accumulate_rows(rows, slots, spans, src_ref, live_ref, lcol_ref, pcol_ref, a_ref, buf_ref, pt_ref, out_ref, acc_ref)


def side_kernel(rows, slots, src_ref, live_ref, lcol_ref, pcol_ref, a_ref, lower_ref, upper_ref, pt_ref, prior_ref, out_ref, buf_ref, acc_ref, sems):
    half = lower_ref.shape[0]
    bs = lower_ref.shape[-1]
    copies = []
    for p in range(2):
        lanes = pl.ds(p * bs, bs)
        copies.append(
            pltpu.make_async_copy(lower_ref.at[:, p], buf_ref.at[pl.ds(0, half), :, lanes], sems.at[2 * p])
        )
        copies.append(
            pltpu.make_async_copy(upper_ref.at[:, p], buf_ref.at[pl.ds(half, half), :, lanes], sems.at[2 * p + 1])
        )
    for cp in copies:
        cp.start()
    out_ref[...] = prior_ref[...]
    for cp in copies:
        cp.wait()
    spans = ((0, CG), (2 * CG, 3 * CG))
    accumulate_rows(rows, slots, spans, src_ref, live_ref, lcol_ref, pcol_ref, a_ref, buf_ref, pt_ref, out_ref, acc_ref)


def pick_kernel(up_sel, down_sel, group_ref, up_ref, down_ref, sems):
    count = up_sel.shape[0]
    copies = []
    for q in range(count):
        copies.append(pltpu.make_async_copy(group_ref.at[up_sel[q]], up_ref.at[q], sems.at[q]))
        copies.append(
            pltpu.make_async_copy(group_ref.at[down_sel[q]], down_ref.at[q], sems.at[count + q])
        )
    for cp in copies:
        cp.start()
    for cp in copies:
        cp.wait()


SMEM = pl.BlockSpec(memory_space=pltpu.SMEM)
VMEM = pl.BlockSpec(memory_space=pltpu.VMEM)
ANY = pl.BlockSpec(memory_space=pl.ANY)


def cost(a_tiles, width, extra_bytes):
    rows, slots, bs, _ = a_tiles.shape
    flops = 2 * rows * slots * 2 * bs ** 3 + 2 * rows * 2 * bs * bs * width * bs
    return pl.CostEstimate(
        flops=flops,
        bytes_accessed=a_tiles.size * 2 + extra_bytes + CG * bs * width * bs * 4,
        transcendentals=0,
    )


def middle_product(a_tiles, group_tiles, p_t, sel, src, live, lcol, pcol):
    rows, slots, bs, _ = a_tiles.shape
    count = sel.shape[0]
    width = 3 * CG
    return pl.pallas_call(
        functools.partial(middle_kernel, rows, slots),
        out_shape=jax.ShapeDtypeStruct((CG, bs, width * bs), jnp.float32),
        in_specs=[SMEM, SMEM, SMEM, SMEM, SMEM, VMEM, ANY, VMEM],
        out_specs=VMEM,
        scratch_shapes=[
            pltpu.VMEM((rows + count, bs, 2 * bs), jnp.bfloat16),
            pltpu.VMEM((bs, width * bs), jnp.float32),
            pltpu.SemaphoreType.DMA((2 * (count + 1),)),
        ],
        compiler_params=pltpu.CompilerParams(vmem_limit_bytes=VMEM_LIMIT),
        cost_estimate=cost(a_tiles, width, (rows + count) * 2 * bs * bs * 2),
    )(src, live, lcol, pcol, sel, a_tiles, group_tiles, p_t)


def side_product(a_tiles, lower, upper, p_t, src, live, lcol, pcol, prior):
    rows, slots, bs, _ = a_tiles.shape
    count = lower.shape[0]
    width = 3 * CG
    return pl.pallas_call(
        functools.partial(side_kernel, rows, slots),
        out_shape=jax.ShapeDtypeStruct((CG, bs, width * bs), jnp.float32),
        in_specs=[SMEM, SMEM, SMEM, SMEM, VMEM, ANY, ANY, VMEM, VMEM],
        input_output_aliases={8: 0},
        out_specs=VMEM,
        scratch_shapes=[
            pltpu.VMEM((2 * count, bs, 2 * bs), jnp.bfloat16),
            pltpu.VMEM((bs, width * bs), jnp.float32),
            pltpu.SemaphoreType.DMA((4,)),
        ],
        compiler_params=pltpu.CompilerParams(vmem_limit_bytes=VMEM_LIMIT),
        cost_estimate=cost(a_tiles, width, 2 * count * 2 * bs * bs * 2),
    )(src, live, lcol, pcol, a_tiles, lower, upper, p_t, prior)


def pick_rows(group_tiles, up_sel, down_sel):
    count = up_sel.shape[0]
    shape = (count,) + group_tiles.shape[1:]
    out = jax.ShapeDtypeStruct(shape, group_tiles.dtype)
    nbytes = 2 * 2 * count * group_tiles[0].size * 2
    return pl.pallas_call(
        pick_kernel,
        out_shape=(out, out),
        in_specs=[SMEM, SMEM, ANY],
        out_specs=(VMEM, VMEM),
        scratch_shapes=[pltpu.SemaphoreType.DMA((2 * count,))],
        compiler_params=pltpu.CompilerParams(vmem_limit_bytes=VMEM_LIMIT),
        cost_estimate=pl.CostEstimate(flops=0, bytes_accessed=nbytes, transcendentals=0),
    )(up_sel, down_sel, group_tiles)


def body(a_tiles, a_cols, p_tiles, p_cols, send_list):
    z_count = lax.axis_size("z")
    core_count = lax.axis_size("core")
    col_count = z_count * core_count
    row_count = lax.axis_size("row")
    g = lax.axis_index("row")
    c = lax.axis_index("z") * core_count + lax.axis_index("core")
    own_rows, slot_count = a_cols.shape
    tile_count = p_cols.shape[1]
    block_size = a_tiles.shape[-1]

    ints = jnp.concatenate([p_cols.reshape(-1), send_list.reshape(-1)])
    group_ints = lax.all_gather(ints, ("z", "core"))
    group_pcols = group_ints[:, : own_rows * tile_count].reshape(-1, tile_count)
    group_send = group_ints[:, own_rows * tile_count :]
    group_tiles = lax.all_gather(p_tiles, ("z", "core"), tiled=True)

    q = jnp.arange(col_count, dtype=jnp.int32)
    base = q * own_rows

    def selection(t):
        return base + jnp.clip(group_send[:, 3 * c + t], 0, own_rows - 1)

    up_sel, mid_sel, down_sel = selection(0), selection(1), selection(2)
    up_tiles, down_tiles = pick_rows(group_tiles, up_sel, down_sel)

    def cols_of(t):
        return group_pcols[q * own_rows + jnp.clip(group_send[:, 3 * c + t], 0, own_rows - 1)]

    lower_tiles, lower_cols = from_behind((up_tiles, cols_of(0)), "row", 1)
    upper_tiles, upper_cols = from_behind((down_tiles, cols_of(2)), "row", -1)
    mid_cols = cols_of(1)

    b = a_cols.reshape(-1)
    live = b >= 0
    bb = jnp.clip(b, 0, own_rows + 3 * col_count - 1)
    is_own = bb < own_rows
    ghost = jnp.maximum(bb - own_rows, 0)
    ghost_q = ghost // 3
    stream = ghost % 3
    src_group = g + stream - 1
    in_range = (src_group >= 0) & (src_group < row_count)
    pcol = jnp.clip(p_cols, 0, CG - 1)

    mid_src = jnp.where(is_own, bb, own_rows + ghost_q)
    mid_live = (live & (is_own | (stream == 1))).astype(jnp.int32)
    mid_table = jnp.concatenate([pcol, jnp.clip(mid_cols, 0, CG - 1)], axis=0) + CG
    mid_lcol = mid_table[mid_src].reshape(-1)

    side_src = jnp.where(stream == 0, ghost_q, col_count + ghost_q)
    side_live = (live & ~is_own & (stream != 1) & in_range).astype(jnp.int32)
    side_table = jnp.concatenate(
        [jnp.clip(lower_cols, 0, CG - 1), jnp.clip(upper_cols, 0, CG - 1) + 2 * CG], axis=0
    )
    side_lcol = side_table[side_src].reshape(-1)

    p_t = jnp.swapaxes(p_tiles, -1, -2)
    pcol = pcol.reshape(-1)
    mid = middle_product(a_tiles, group_tiles, p_t, mid_sel, mid_src, mid_live, mid_lcol, pcol)
    partial = side_product(
        a_tiles, lower_tiles, upper_tiles, p_t, side_src, side_live, side_lcol, pcol, mid
    )
    partial = partial.reshape(CG * block_size, 3 * CG * block_size)
    partial = lax.psum_scatter(partial, "z", scatter_dimension=0, tiled=True)
    k = lax.axis_index("core")
    half = partial.shape[0] // 2
    mine = lax.dynamic_slice_in_dim(partial, k * half, half, axis=0)
    other = lax.dynamic_slice_in_dim(partial, (1 - k) * half, half, axis=0)
    return mine + lax.ppermute(other, "core", [(0, 1), (1, 0)])


def solution(mesh):
    rows, cols = mesh.devices.shape
    chip_mesh = jax.sharding.Mesh(mesh.devices.reshape(rows, cols // 2, 2), ("row", "z", "core"))
    split = ("row", "z", "core")
    in_specs = (
        P(split, None, None, None),
        P(split, None),
        P(split, None, None, None),
        P(split, None),
        P(split, None),
    )
    out_specs = P(split, None)
    return jax.shard_map(body, mesh=chip_mesh, in_specs=in_specs, out_specs=out_specs, check_vma=False)
```

```python
import functools

import jax
import jax.numpy as jnp
from jax import lax
from jax.experimental import pallas as pl
from jax.experimental.pallas import tpu as pltpu
from jax.sharding import PartitionSpec as P

CG = 4
VMEM_LIMIT = 60 * 1024 * 1024


def from_behind(value, axis, steps):
    count = lax.axis_size(axis)
    leading, last = (max(0, -steps), min(count, count - steps))
    return lax.ppermute(value, axis, [(source, source + steps) for source in range(leading, last)])


def accumulate_rows(rows, slots, spans, src_ref, live_ref, lcol_ref, pcol_ref, a_ref, b_ref, pt_ref, out_ref, acc_ref):
    bs = a_ref.shape[-1]
    for i in range(rows):
        for lo, hi in spans:
            acc_ref[:, lo * bs : hi * bs] = jnp.zeros((bs, (hi - lo) * bs), jnp.float32)

        def slot(k, carry):
            s = i * slots + k

            @pl.when(live_ref[s] != 0)
            def _():
                src = src_ref[s]
                both = jnp.dot(a_ref[i, k], b_ref[src], preferred_element_type=jnp.float32)
                for p in range(2):
                    col = pl.multiple_of(lcol_ref[2 * s + p] * bs, bs)
                    acc_ref[:, pl.ds(col, bs)] += both[:, p * bs : (p + 1) * bs]

            return carry

        lax.fori_loop(0, slots, slot, 0)
        for lo, hi in spans:
            prod = acc_ref[:, lo * bs : hi * bs].astype(jnp.bfloat16)
            for p in range(2):
                m = pcol_ref[2 * i + p]
                out_ref[m, :, lo * bs : hi * bs] += jnp.dot(
                    pt_ref[i, p], prod, preferred_element_type=jnp.float32
                )


def middle_kernel(rows, slots, src_ref, live_ref, lcol_ref, pcol_ref, sel_ref, a_ref, group_ref, pt_ref, out_ref, buf_ref, acc_ref, sems):
    count = sel_ref.shape[0]
    own = buf_ref.shape[0] - count
    bs = group_ref.shape[-1]
    me = lax.axis_index("z") * lax.axis_size("core") + lax.axis_index("core")
    copies = []
    for p in range(2):
        base = p * (count + 1)
        lanes = pl.ds(p * bs, bs)
        copies.append(
            pltpu.make_async_copy(group_ref.at[pl.ds(me * own, own), p], buf_ref.at[pl.ds(0, own), :, lanes], sems.at[base])
        )
        for q in range(count):
            copies.append(
                pltpu.make_async_copy(group_ref.at[sel_ref[q], p], buf_ref.at[own + q, :, lanes], sems.at[base + q + 1])
            )
    for cp in copies:
        cp.start()
    out_ref[...] = jnp.zeros_like(out_ref)
    for cp in copies:
        cp.wait()
    spans = ((CG, 2 * CG),)
    accumulate_rows(rows, slots, spans, src_ref, live_ref, lcol_ref, pcol_ref, a_ref, buf_ref, pt_ref, out_ref, acc_ref)


def side_kernel(rows, slots, src_ref, live_ref, lcol_ref, pcol_ref, a_ref, lower_a, lower_b, upper_a, upper_b, pt_ref, prior_ref, out_ref, buf_ref, acc_ref, sems):
    part = lower_a.shape[0]
    bs = lower_a.shape[-1]
    copies = []
    for n, piece in enumerate((lower_a, lower_b, upper_a, upper_b)):
        for p in range(2):
            lanes = pl.ds(p * bs, bs)
            copies.append(
                pltpu.make_async_copy(piece.at[:, p], buf_ref.at[pl.ds(n * part, part), :, lanes], sems.at[2 * n + p])
            )
    for cp in copies:
        cp.start()
    out_ref[...] = prior_ref[...]
    for cp in copies:
        cp.wait()
    spans = ((0, CG), (2 * CG, 3 * CG))
    accumulate_rows(rows, slots, spans, src_ref, live_ref, lcol_ref, pcol_ref, a_ref, buf_ref, pt_ref, out_ref, acc_ref)


def pick_kernel(up_sel, down_sel, group_ref, up_ref, down_ref, sems):
    count = up_sel.shape[0]
    copies = []
    for q in range(count):
        copies.append(pltpu.make_async_copy(group_ref.at[up_sel[q]], up_ref.at[q], sems.at[q]))
        copies.append(
            pltpu.make_async_copy(group_ref.at[down_sel[q]], down_ref.at[q], sems.at[count + q])
        )
    for cp in copies:
        cp.start()
    for cp in copies:
        cp.wait()


SMEM = pl.BlockSpec(memory_space=pltpu.SMEM)
VMEM = pl.BlockSpec(memory_space=pltpu.VMEM)
ANY = pl.BlockSpec(memory_space=pl.ANY)


def cost(a_tiles, width, extra_bytes):
    rows, slots, bs, _ = a_tiles.shape
    flops = 2 * rows * slots * 2 * bs ** 3 + 2 * rows * 2 * bs * bs * width * bs
    return pl.CostEstimate(
        flops=flops,
        bytes_accessed=a_tiles.size * 2 + extra_bytes + CG * bs * width * bs * 4,
        transcendentals=0,
    )


def middle_product(a_tiles, group_tiles, p_t, sel, src, live, lcol, pcol):
    rows, slots, bs, _ = a_tiles.shape
    count = sel.shape[0]
    width = 3 * CG
    return pl.pallas_call(
        functools.partial(middle_kernel, rows, slots),
        out_shape=jax.ShapeDtypeStruct((CG, bs, width * bs), jnp.float32),
        in_specs=[SMEM, SMEM, SMEM, SMEM, SMEM, VMEM, ANY, VMEM],
        out_specs=VMEM,
        scratch_shapes=[
            pltpu.VMEM((rows + count, bs, 2 * bs), jnp.bfloat16),
            pltpu.VMEM((bs, width * bs), jnp.float32),
            pltpu.SemaphoreType.DMA((2 * (count + 1),)),
        ],
        compiler_params=pltpu.CompilerParams(vmem_limit_bytes=VMEM_LIMIT),
        cost_estimate=cost(a_tiles, width, (rows + count) * 2 * bs * bs * 2),
    )(src, live, lcol, pcol, sel, a_tiles, group_tiles, p_t)


def side_product(a_tiles, lower, upper, p_t, src, live, lcol, pcol, prior):
    rows, slots, bs, _ = a_tiles.shape
    count = 2 * lower[0].shape[0]
    width = 3 * CG
    return pl.pallas_call(
        functools.partial(side_kernel, rows, slots),
        out_shape=jax.ShapeDtypeStruct((CG, bs, width * bs), jnp.float32),
        in_specs=[SMEM, SMEM, SMEM, SMEM, VMEM, ANY, ANY, ANY, ANY, VMEM, VMEM],
        input_output_aliases={10: 0},
        out_specs=VMEM,
        scratch_shapes=[
            pltpu.VMEM((2 * count, bs, 2 * bs), jnp.bfloat16),
            pltpu.VMEM((bs, width * bs), jnp.float32),
            pltpu.SemaphoreType.DMA((8,)),
        ],
        compiler_params=pltpu.CompilerParams(vmem_limit_bytes=VMEM_LIMIT),
        cost_estimate=cost(a_tiles, width, 2 * count * 2 * bs * bs * 2),
    )(src, live, lcol, pcol, a_tiles, *lower, *upper, p_t, prior)


def pick_rows(group_tiles, up_sel, down_sel):
    count = up_sel.shape[0]
    shape = (count,) + group_tiles.shape[1:]
    out = jax.ShapeDtypeStruct(shape, group_tiles.dtype)
    nbytes = 2 * 2 * count * group_tiles[0].size * 2
    return pl.pallas_call(
        pick_kernel,
        out_shape=(out, out),
        in_specs=[SMEM, SMEM, ANY],
        out_specs=(VMEM, VMEM),
        scratch_shapes=[pltpu.SemaphoreType.DMA((2 * count,))],
        compiler_params=pltpu.CompilerParams(vmem_limit_bytes=VMEM_LIMIT),
        cost_estimate=pl.CostEstimate(flops=0, bytes_accessed=nbytes, transcendentals=0),
    )(up_sel, down_sel, group_tiles)


def body(a_tiles, a_cols, p_tiles, p_cols, send_list):
    z_count = lax.axis_size("z")
    core_count = lax.axis_size("core")
    col_count = z_count * core_count
    row_count = lax.axis_size("row")
    g = lax.axis_index("row")
    c = lax.axis_index("z") * core_count + lax.axis_index("core")
    own_rows, slot_count = a_cols.shape
    tile_count = p_cols.shape[1]
    block_size = a_tiles.shape[-1]

    ints = jnp.concatenate([p_cols.reshape(-1), send_list.reshape(-1)])
    group_ints = lax.all_gather(ints, ("z", "core"))
    group_pcols = group_ints[:, : own_rows * tile_count].reshape(-1, tile_count)
    group_send = group_ints[:, own_rows * tile_count :]
    group_tiles = lax.all_gather(p_tiles, ("z", "core"), tiled=True)

    q = jnp.arange(col_count, dtype=jnp.int32)
    base = q * own_rows

    def selection(t):
        return base + jnp.clip(group_send[:, 3 * c + t], 0, own_rows - 1)

    up_sel, mid_sel, down_sel = selection(0), selection(1), selection(2)
    half = col_count // 2
    up_a, down_a = pick_rows(group_tiles, up_sel[:half], down_sel[:half])
    lower_a, upper_a = from_behind(up_a, "row", 1), from_behind(down_a, "row", -1)
    later_up, later_down, up_a = lax.optimization_barrier((up_sel[half:], down_sel[half:], up_a))
    up_b, down_b = pick_rows(group_tiles, later_up, later_down)
    lower_b, upper_b = from_behind(up_b, "row", 1), from_behind(down_b, "row", -1)

    def cols_of(t):
        return group_pcols[q * own_rows + jnp.clip(group_send[:, 3 * c + t], 0, own_rows - 1)]

    lower_cols = from_behind(cols_of(0), "row", 1)
    upper_cols = from_behind(cols_of(2), "row", -1)
    mid_cols = cols_of(1)

    b = a_cols.reshape(-1)
    live = b >= 0
    bb = jnp.clip(b, 0, own_rows + 3 * col_count - 1)
    is_own = bb < own_rows
    ghost = jnp.maximum(bb - own_rows, 0)
    ghost_q = ghost // 3
    stream = ghost % 3
    src_group = g + stream - 1
    in_range = (src_group >= 0) & (src_group < row_count)
    pcol = jnp.clip(p_cols, 0, CG - 1)

    mid_src = jnp.where(is_own, bb, own_rows + ghost_q)
    mid_live = (live & (is_own | (stream == 1))).astype(jnp.int32)
    mid_table = jnp.concatenate([pcol, jnp.clip(mid_cols, 0, CG - 1)], axis=0) + CG
    mid_lcol = mid_table[mid_src].reshape(-1)

    side_src = jnp.where(stream == 0, ghost_q, col_count + ghost_q)
    side_live = (live & ~is_own & (stream != 1) & in_range).astype(jnp.int32)
    side_table = jnp.concatenate(
        [jnp.clip(lower_cols, 0, CG - 1), jnp.clip(upper_cols, 0, CG - 1) + 2 * CG], axis=0
    )
    side_lcol = side_table[side_src].reshape(-1)

    p_t = jnp.swapaxes(p_tiles, -1, -2)
    pcol = pcol.reshape(-1)
    mid = middle_product(a_tiles, group_tiles, p_t, mid_sel, mid_src, mid_live, mid_lcol, pcol)
    partial = side_product(
        a_tiles, (lower_a, lower_b), (upper_a, upper_b), p_t, side_src, side_live, side_lcol, pcol, mid
    )
    partial = partial.reshape(CG * block_size, 3 * CG * block_size)
    partial = lax.psum_scatter(partial, "z", scatter_dimension=0, tiled=True)
    k = lax.axis_index("core")
    half = partial.shape[0] // 2
    mine = lax.dynamic_slice_in_dim(partial, k * half, half, axis=0)
    other = lax.dynamic_slice_in_dim(partial, (1 - k) * half, half, axis=0)
    return mine + lax.ppermute(other, "core", [(0, 1), (1, 0)])


def solution(mesh):
    rows, cols = mesh.devices.shape
    chip_mesh = jax.sharding.Mesh(mesh.devices.reshape(rows, cols // 2, 2), ("row", "z", "core"))
    split = ("row", "z", "core")
    in_specs = (
        P(split, None, None, None),
        P(split, None),
        P(split, None, None, None),
        P(split, None),
        P(split, None),
    )
    out_specs = P(split, None)
    return jax.shard_map(body, mesh=chip_mesh, in_specs=in_specs, out_specs=out_specs, check_vma=False)
```

```python
import functools

import jax
import jax.numpy as jnp
from jax import lax
from jax.experimental import pallas as pl
from jax.experimental.pallas import tpu as pltpu
from jax.sharding import PartitionSpec as P

CG = 4
VMEM_LIMIT = 60 * 1024 * 1024


def from_behind(value, axis, steps):
    count = lax.axis_size(axis)
    leading, last = (max(0, -steps), min(count, count - steps))
    return lax.ppermute(value, axis, [(source, source + steps) for source in range(leading, last)])


def accumulate_rows(rows, slots, spans, src_ref, live_ref, lcol_ref, pcol_ref, a_ref, b_ref, pt_ref, out_ref, acc_ref):
    bs = a_ref.shape[-1]
    for i in range(rows):
        for lo, hi in spans:
            acc_ref[:, lo * bs : hi * bs] = jnp.zeros((bs, (hi - lo) * bs), jnp.float32)

        def slot(k, carry):
            s = i * slots + k

            @pl.when(live_ref[s] != 0)
            def _():
                src = src_ref[s]
                both = jnp.dot(a_ref[i, k], b_ref[src], preferred_element_type=jnp.float32)
                for p in range(2):
                    col = pl.multiple_of(lcol_ref[2 * s + p] * bs, bs)
                    acc_ref[:, pl.ds(col, bs)] += both[:, p * bs : (p + 1) * bs]

            return carry

        lax.fori_loop(0, slots, slot, 0)
        for lo, hi in spans:
            prod = acc_ref[:, lo * bs : hi * bs].astype(jnp.bfloat16)
            for p in range(2):
                m = pcol_ref[2 * i + p]
                out_ref[m, :, lo * bs : hi * bs] += jnp.dot(
                    pt_ref[i, p], prod, preferred_element_type=jnp.float32
                )


def middle_kernel(rows, slots, src_ref, live_ref, lcol_ref, pcol_ref, sel_ref, a_ref, group_ref, pt_ref, out_ref, buf_ref, acc_ref, sems):
    count = sel_ref.shape[0]
    own = buf_ref.shape[0] - count
    bs = group_ref.shape[-1]
    me = lax.axis_index("z") * lax.axis_size("core") + lax.axis_index("core")
    copies = []
    for p in range(2):
        base = p * (count + 1)
        lanes = pl.ds(p * bs, bs)
        copies.append(
            pltpu.make_async_copy(group_ref.at[pl.ds(me * own, own), p], buf_ref.at[pl.ds(0, own), :, lanes], sems.at[base])
        )
        for q in range(count):
            copies.append(
                pltpu.make_async_copy(group_ref.at[sel_ref[q], p], buf_ref.at[own + q, :, lanes], sems.at[base + q + 1])
            )
    for cp in copies:
        cp.start()
    out_ref[...] = jnp.zeros_like(out_ref)
    for cp in copies:
        cp.wait()
    spans = ((CG, 2 * CG),)
    accumulate_rows(rows, slots, spans, src_ref, live_ref, lcol_ref, pcol_ref, a_ref, buf_ref, pt_ref, out_ref, acc_ref)


def side_kernel(rows, slots, src_ref, live_ref, lcol_ref, pcol_ref, a_ref, lower_ref, upper_ref, pt_ref, prior_ref, out_ref, buf_ref, acc_ref, sems):
    half = lower_ref.shape[0]
    bs = lower_ref.shape[-1]
    copies = []
    for p in range(2):
        lanes = pl.ds(p * bs, bs)
        copies.append(
            pltpu.make_async_copy(lower_ref.at[:, p], buf_ref.at[pl.ds(0, half), :, lanes], sems.at[2 * p])
        )
        copies.append(
            pltpu.make_async_copy(upper_ref.at[:, p], buf_ref.at[pl.ds(half, half), :, lanes], sems.at[2 * p + 1])
        )
    for cp in copies:
        cp.start()
    out_ref[...] = prior_ref[...]
    for cp in copies:
        cp.wait()
    spans = ((0, CG), (2 * CG, 3 * CG))
    accumulate_rows(rows, slots, spans, src_ref, live_ref, lcol_ref, pcol_ref, a_ref, buf_ref, pt_ref, out_ref, acc_ref)


def pick_kernel(up_sel, down_sel, group_ref, up_ref, down_ref, stage, sems_in, sems_out):
    count = up_sel.shape[0]
    reads, writes = [], []
    for q in range(count):
        for n, (sel, out_ref) in enumerate(((up_sel, up_ref), (down_sel, down_ref))):
            j = n * count + q
            reads.append(pltpu.make_async_copy(group_ref.at[sel[q]], stage.at[j], sems_in.at[j]))
            writes.append(pltpu.make_async_copy(stage.at[j], out_ref.at[q], sems_out.at[j]))
    for cp in reads:
        cp.start()
    for rd, wr in zip(reads, writes):
        rd.wait()
        wr.start()
    for wr in writes:
        wr.wait()


SMEM = pl.BlockSpec(memory_space=pltpu.SMEM)
VMEM = pl.BlockSpec(memory_space=pltpu.VMEM)
ANY = pl.BlockSpec(memory_space=pl.ANY)


def cost(a_tiles, width, extra_bytes):
    rows, slots, bs, _ = a_tiles.shape
    flops = 2 * rows * slots * 2 * bs ** 3 + 2 * rows * 2 * bs * bs * width * bs
    return pl.CostEstimate(
        flops=flops,
        bytes_accessed=a_tiles.size * 2 + extra_bytes + CG * bs * width * bs * 4,
        transcendentals=0,
    )


def middle_product(a_tiles, group_tiles, p_t, sel, src, live, lcol, pcol):
    rows, slots, bs, _ = a_tiles.shape
    count = sel.shape[0]
    width = 3 * CG
    return pl.pallas_call(
        functools.partial(middle_kernel, rows, slots),
        out_shape=jax.ShapeDtypeStruct((CG, bs, width * bs), jnp.float32),
        in_specs=[SMEM, SMEM, SMEM, SMEM, SMEM, VMEM, ANY, VMEM],
        out_specs=VMEM,
        scratch_shapes=[
            pltpu.VMEM((rows + count, bs, 2 * bs), jnp.bfloat16),
            pltpu.VMEM((bs, width * bs), jnp.float32),
            pltpu.SemaphoreType.DMA((2 * (count + 1),)),
        ],
        compiler_params=pltpu.CompilerParams(vmem_limit_bytes=VMEM_LIMIT),
        cost_estimate=cost(a_tiles, width, (rows + count) * 2 * bs * bs * 2),
    )(src, live, lcol, pcol, sel, a_tiles, group_tiles, p_t)


def side_product(a_tiles, lower, upper, p_t, src, live, lcol, pcol, prior):
    rows, slots, bs, _ = a_tiles.shape
    count = lower.shape[0]
    width = 3 * CG
    return pl.pallas_call(
        functools.partial(side_kernel, rows, slots),
        out_shape=jax.ShapeDtypeStruct((CG, bs, width * bs), jnp.float32),
        in_specs=[SMEM, SMEM, SMEM, SMEM, VMEM, ANY, ANY, VMEM, VMEM],
        input_output_aliases={8: 0},
        out_specs=VMEM,
        scratch_shapes=[
            pltpu.VMEM((2 * count, bs, 2 * bs), jnp.bfloat16),
            pltpu.VMEM((bs, width * bs), jnp.float32),
            pltpu.SemaphoreType.DMA((4,)),
        ],
        compiler_params=pltpu.CompilerParams(vmem_limit_bytes=VMEM_LIMIT),
        cost_estimate=cost(a_tiles, width, 2 * count * 2 * bs * bs * 2),
    )(src, live, lcol, pcol, a_tiles, lower, upper, p_t, prior)


def pick_rows(group_tiles, up_sel, down_sel):
    count = up_sel.shape[0]
    shape = (count,) + group_tiles.shape[1:]
    out = jax.ShapeDtypeStruct(shape, group_tiles.dtype)
    nbytes = 2 * 2 * count * group_tiles[0].size * 2
    return pl.pallas_call(
        pick_kernel,
        out_shape=(out, out),
        in_specs=[SMEM, SMEM, ANY],
        out_specs=(ANY, ANY),
        scratch_shapes=[
            pltpu.VMEM((2 * count,) + group_tiles.shape[1:], group_tiles.dtype),
            pltpu.SemaphoreType.DMA((2 * count,)),
            pltpu.SemaphoreType.DMA((2 * count,)),
        ],
        compiler_params=pltpu.CompilerParams(vmem_limit_bytes=VMEM_LIMIT),
        cost_estimate=pl.CostEstimate(flops=0, bytes_accessed=nbytes, transcendentals=0),
    )(up_sel, down_sel, group_tiles)


def body(a_tiles, a_cols, p_tiles, p_cols, send_list):
    z_count = lax.axis_size("z")
    core_count = lax.axis_size("core")
    col_count = z_count * core_count
    row_count = lax.axis_size("row")
    g = lax.axis_index("row")
    c = lax.axis_index("z") * core_count + lax.axis_index("core")
    own_rows, slot_count = a_cols.shape
    tile_count = p_cols.shape[1]
    block_size = a_tiles.shape[-1]

    ints = jnp.concatenate([p_cols.reshape(-1), send_list.reshape(-1)])
    group_ints = lax.all_gather(ints, ("z", "core"))
    group_pcols = group_ints[:, : own_rows * tile_count].reshape(-1, tile_count)
    group_send = group_ints[:, own_rows * tile_count :]
    group_tiles = lax.all_gather(p_tiles, ("z", "core"), tiled=True)

    q = jnp.arange(col_count, dtype=jnp.int32)
    base = q * own_rows

    def selection(t):
        return base + jnp.clip(group_send[:, 3 * c + t], 0, own_rows - 1)

    up_sel, mid_sel, down_sel = selection(0), selection(1), selection(2)
    up_tiles, down_tiles = pick_rows(group_tiles, up_sel, down_sel)

    def cols_of(t):
        return group_pcols[q * own_rows + jnp.clip(group_send[:, 3 * c + t], 0, own_rows - 1)]

    lower_tiles, lower_cols = from_behind((up_tiles, cols_of(0)), "row", 1)
    upper_tiles, upper_cols = from_behind((down_tiles, cols_of(2)), "row", -1)
    mid_cols = cols_of(1)

    b = a_cols.reshape(-1)
    live = b >= 0
    bb = jnp.clip(b, 0, own_rows + 3 * col_count - 1)
    is_own = bb < own_rows
    ghost = jnp.maximum(bb - own_rows, 0)
    ghost_q = ghost // 3
    stream = ghost % 3
    src_group = g + stream - 1
    in_range = (src_group >= 0) & (src_group < row_count)
    pcol = jnp.clip(p_cols, 0, CG - 1)

    mid_src = jnp.where(is_own, bb, own_rows + ghost_q)
    mid_live = (live & (is_own | (stream == 1))).astype(jnp.int32)
    mid_table = jnp.concatenate([pcol, jnp.clip(mid_cols, 0, CG - 1)], axis=0) + CG
    mid_lcol = mid_table[mid_src].reshape(-1)

    side_src = jnp.where(stream == 0, ghost_q, col_count + ghost_q)
    side_live = (live & ~is_own & (stream != 1) & in_range).astype(jnp.int32)
    side_table = jnp.concatenate(
        [jnp.clip(lower_cols, 0, CG - 1), jnp.clip(upper_cols, 0, CG - 1) + 2 * CG], axis=0
    )
    side_lcol = side_table[side_src].reshape(-1)

    p_t = jnp.swapaxes(p_tiles, -1, -2)
    pcol = pcol.reshape(-1)
    mid = middle_product(a_tiles, group_tiles, p_t, mid_sel, mid_src, mid_live, mid_lcol, pcol)
    partial = side_product(
        a_tiles, lower_tiles, upper_tiles, p_t, side_src, side_live, side_lcol, pcol, mid
    )
    partial = partial.reshape(CG * block_size, 3 * CG * block_size)
    partial = lax.psum_scatter(partial, "z", scatter_dimension=0, tiled=True)
    k = lax.axis_index("core")
    half = partial.shape[0] // 2
    mine = lax.dynamic_slice_in_dim(partial, k * half, half, axis=0)
    other = lax.dynamic_slice_in_dim(partial, (1 - k) * half, half, axis=0)
    return mine + lax.ppermute(other, "core", [(0, 1), (1, 0)])


def solution(mesh):
    rows, cols = mesh.devices.shape
    chip_mesh = jax.sharding.Mesh(mesh.devices.reshape(rows, cols // 2, 2), ("row", "z", "core"))
    split = ("row", "z", "core")
    in_specs = (
        P(split, None, None, None),
        P(split, None),
        P(split, None, None, None),
        P(split, None),
        P(split, None),
    )
    out_specs = P(split, None)
    return jax.shard_map(body, mesh=chip_mesh, in_specs=in_specs, out_specs=out_specs, check_vma=False)
```
